128 devices in a mesh: seq: 16 (over z_lo, x, core), zero: 8 (over y, z_hi).
Axes of the slice: x: 4, y: 4, z: 4 (z_hi: 2, z_lo: 2; z = z_hi * 2 + z_lo), core: 2. Of those that a mesh axis runs over, the one named last changes fastest.
Arguments:
- tokens: bfloat16 [16384, 1024], P(('seq', 'zero')), may hold values from -18 to 18
- projection: bfloat16 [1024, 3072], P('zero'), may hold values from -0.1875 to 0.1875
- pattern: int32 [128, 8], replicated, may hold values from 0 to 127, as said below
- upstream: bfloat16 [16384, 1024], P(('seq', 'zero')), may hold values from -6 to 6
Outputs:
- attended: bfloat16 [16384, 1024], P(('seq', 'zero'))
- token_gradient: bfloat16 [16384, 1024], P(('seq', 'zero'))
- weight_gradient: float32 [1024, 3072], P('zero')
The draws below stay inside these ranges and needn't reach their ends.
Inputs may be any that keep to these rules, and one draw needn't show every extreme that they name: `pattern`: each row names 8 different key blocks, block 0 and the row's own block among them.
All inputs are finite; a program needn't handle non-finite values.
Results may differ from the reference program's by a relative error of at most 0.01.
The reference program's roundings to bfloat16 on the way count: a program that leaves them out, or rounds other values in their place, can miss the bound.
Values may be sent and summed in bfloat16 or wider, within the bound.
No kernel may reach another device: no remote copies, remote signals or barrier semaphores. Data moves between devices by JAX's collectives and lax.ppermute only.
A program may use at most 128 MiB of HBM per device.

```python
import jax
import jax.numpy as jnp
from jax import lax

D = 1024
HEADS = 16
HEAD = 64
BLOCK = 128
NBK = 8
TOK_DEV = 128
HD = 1024
TOKENS = 16384
N_ZERO = 8


def draw_tokens(key, part):
    base_key = jax.random.fold_in(key, 11)
    spike_key = jax.random.fold_in(key, 12)
    spike_width = D // 8
    shard_count = TOKENS // TOK_DEV
    chosen = jax.random.randint(spike_key, (shard_count, 1), 0, 8)
    column_block = (jnp.arange(D) // spike_width)[None, :]
    spike_gain = jnp.where(column_block == chosen, 3.0, 1.0).astype(jnp.float32)
    spike_gain = jnp.repeat(spike_gain, TOK_DEV, axis=0)
    base_values = jnp.clip(jax.random.normal(base_key, (TOKENS, D), jnp.float32), -6.0, 6.0)
    return (base_values * spike_gain).astype(jnp.bfloat16)


def draw_pattern(key, part):
    row_total = TOKENS // BLOCK
    row_index = jnp.arange(row_total, dtype=jnp.int32)[:, None]
    column_index = jnp.arange(row_total, dtype=jnp.int32)[None, :]
    noise_bits = jax.random.randint(jax.random.fold_in(key, 21), (row_total, row_total), 0, 1 << 16, dtype=jnp.int32)
    forced = (column_index == 0) | (jnp.abs(column_index - row_index) <= 1)
    priority = jnp.where(forced, 1 << 17, noise_bits) * row_total + column_index
    picked = lax.top_k(priority, NBK)[1]
    return picked.astype(jnp.int32)


def shard_levels(stream_key, shape, split, smallest, largest):
    loudness = 1.0
    for axis_at, shards_of in split:
        steps = jax.random.uniform(jax.random.fold_in(jax.random.fold_in(stream_key, 6), axis_at), (shards_of,), jnp.float32, smallest / len(split), largest / len(split))
        loudness = loudness * jnp.repeat(jnp.exp(steps), shape[axis_at] // shards_of).reshape((-1,) + (1,) * (len(shape) - 1 - axis_at))
    return loudness


def noise(stream_key, extent, deviation, reach, shards=(), held_as=jnp.bfloat16):
    drawn = deviation * jax.random.normal(stream_key, extent, jnp.float32)
    if shards:
        drawn = drawn * shard_levels(stream_key, extent, shards, -0.22, 0.18)
    return jnp.clip(drawn, -reach, reach).astype(held_as)


def setup_inputs(seed: int = 0) -> dict:
    key_of = jax.random.split(jax.random.key(seed), 5)
    tokens = draw_tokens(jax.random.fold_in(key_of[4], 71), 0)
    projection = noise(key_of[1], (D, 3 * HD), D ** -0.5, 0.1875, ((0, 8),))
    pattern = draw_pattern(jax.random.fold_in(key_of[4], 71), 0)
    upstream = noise(key_of[3], (TOKENS, HD), 1.0, 6.0, ((0, 128),))
    return {"tokens": tokens, "projection": projection, "pattern": pattern, "upstream": upstream}


def reference(tokens, projection, pattern, upstream):
    score_scale = HEAD ** -0.5
    row_blocks = TOKENS // BLOCK
    per_shard = TOK_DEV // BLOCK
    projected = jnp.dot(tokens, projection, preferred_element_type=jnp.float32).astype(jnp.bfloat16)
    head_slabs = jnp.moveaxis(projected.reshape(row_blocks, BLOCK, 3, HEADS, HEAD), 3, 0)
    head_upstream = jnp.moveaxis(upstream.reshape(row_blocks, BLOCK, HEADS, HEAD), 2, 0)
    owners = ((jnp.arange(row_blocks) // per_shard) % N_ZERO).astype(jnp.int32)

    def group_sum(terms):
        grouped = jnp.zeros((N_ZERO, row_blocks, BLOCK, HEAD), jnp.float32).at[owners[:, None], pattern].add(terms)
        rounded = lax.optimization_barrier(grouped.astype(jnp.bfloat16)).astype(jnp.float32)
        return jnp.sum(rounded, axis=0).astype(jnp.bfloat16)

    def one_head(packed):
        head_slab, slab_upstream = packed
        queries = head_slab[:, :, 0].astype(jnp.float32)
        key_rows = head_slab[:, :, 1]
        value_rows = head_slab[:, :, 2]
        key_chosen = key_rows[pattern].reshape(row_blocks, NBK * BLOCK, HEAD).astype(jnp.float32)
        value_chosen = value_rows[pattern].reshape(row_blocks, NBK * BLOCK, HEAD).astype(jnp.float32)
        scores = jnp.einsum("rqe,rke->rqk", queries, key_chosen) * score_scale
        row_max = jnp.max(scores, axis=-1, keepdims=True)
        exponent = jnp.exp(scores - row_max)
        prob_full = exponent / jnp.sum(exponent, axis=-1, keepdims=True)
        prob_low = lax.optimization_barrier(prob_full.astype(jnp.bfloat16)).astype(jnp.float32)
        attended = jnp.einsum("rqk,rke->rqe", prob_low, value_chosen).astype(jnp.bfloat16)
        upstream_full = slab_upstream.astype(jnp.float32)
        prob_grad = jnp.einsum("rqe,rke->rqk", upstream_full, value_chosen)
        row_delta = jnp.sum(prob_full * prob_grad, axis=-1, keepdims=True)
        score_grad = lax.optimization_barrier((prob_full * (prob_grad - row_delta) * score_scale).astype(jnp.bfloat16)).astype(jnp.float32)
        query_grad = jnp.einsum("rqk,rke->rqe", score_grad, key_chosen).astype(jnp.bfloat16)
        key_terms = jnp.einsum("rqk,rqe->rke", score_grad, queries).reshape(row_blocks, NBK, BLOCK, HEAD)
        value_terms = jnp.einsum("rqk,rqe->rke", prob_low, upstream_full).reshape(row_blocks, NBK, BLOCK, HEAD)
        return attended, query_grad, group_sum(key_terms), group_sum(value_terms)

    attended_all, query_all, key_all, value_all = lax.map(one_head, (head_slabs, head_upstream))
    attended_out = jnp.moveaxis(attended_all, 0, 2).reshape(TOKENS, HD)
    stacked = jnp.stack([query_all, key_all, value_all], axis=0)
    projected_gradient = jnp.transpose(stacked, (2, 3, 0, 1, 4)).reshape(TOKENS, 3 * HD)
    token_gradient = jnp.dot(projected_gradient, projection.T, preferred_element_type=jnp.float32).astype(jnp.bfloat16)
    weight_gradient = jnp.dot(tokens.T, projected_gradient, preferred_element_type=jnp.float32)
    return attended_out, token_gradient, weight_gradient
```

```python
import jax
import jax.numpy as jnp
from jax import lax
from jax.sharding import PartitionSpec as P

HEADS = 16
HEAD = 64
BLOCK = 128
NBK = 8


def on_device(tokens, projection, pattern, upstream):
    seq_count = lax.axis_size("seq")
    zero_count = lax.axis_size("zero")
    zero_index = lax.axis_index("zero")
    tok_rows = tokens.shape[0]
    model_width = tokens.shape[1]
    heads_here = HEADS // seq_count
    head_cols = heads_here * HEAD
    per_shard = tok_rows // BLOCK
    local_blocks = seq_count * per_shard
    group_size = 4
    step_count = local_blocks // group_size
    score_scale = HEAD ** (-0.5)
    weights = lax.all_gather(projection, "zero", axis=0, tiled=True)
    projected = jnp.dot(tokens, weights, preferred_element_type=jnp.float32).astype(jnp.bfloat16)
    projected = projected.reshape(tok_rows, 3, seq_count, head_cols)
    by_head = lax.all_to_all(projected, "seq", split_axis=2, concat_axis=0, tiled=True)
    by_head = by_head.reshape(local_blocks * BLOCK, 3, head_cols)
    key_all, value_all = (
        lax.all_gather(by_head[:, 1], "zero", axis=0, tiled=True),
        lax.all_gather(by_head[:, 2], "zero", axis=0, tiled=True),
    )
    key_all = key_all.reshape(zero_count * local_blocks, BLOCK, heads_here, HEAD)
    value_all = value_all.reshape(zero_count * local_blocks, BLOCK, heads_here, HEAD)
    queries = by_head[:, 0].reshape(step_count, group_size, BLOCK, heads_here, HEAD)
    incoming = lax.all_to_all(
        upstream.reshape(tok_rows, seq_count, head_cols),
        "seq",
        split_axis=1,
        concat_axis=0,
        tiled=True,
    )
    incoming = incoming.reshape(step_count, group_size, BLOCK, heads_here, HEAD)
    local_ids = jnp.arange(local_blocks, dtype=jnp.int32)
    row_ids = (local_ids // per_shard * zero_count + zero_index) * per_shard + local_ids % per_shard
    row_lists = pattern[row_ids]
    shard_ids = row_lists // per_shard
    key_slots = (
        shard_ids % zero_count * local_blocks
        + shard_ids // zero_count * per_shard
        + row_lists % per_shard
    )
    key_slots = key_slots.reshape(step_count, group_size, NBK)

    def attend(carried, inputs):
        key_grad, value_grad = carried
        query_block, up_block, slot_block = inputs
        key_chosen = key_all[slot_block].reshape(group_size, NBK * BLOCK, heads_here, HEAD)
        value_chosen = value_all[slot_block].reshape(group_size, NBK * BLOCK, heads_here, HEAD)
        scores = (
            jnp.einsum(
                "rqhe,rkhe->rhqk", query_block, key_chosen, preferred_element_type=jnp.float32
            )
            * score_scale
        )
        row_max = jnp.max(scores, axis=-1, keepdims=True)
        exponent = jnp.exp(scores - row_max)
        prob_full = exponent / jnp.sum(exponent, axis=-1, keepdims=True)
        prob_low = prob_full.astype(jnp.bfloat16)
        out_block = jnp.einsum(
            "rhqk,rkhe->rqhe", prob_low, value_chosen, preferred_element_type=jnp.float32
        ).astype(jnp.bfloat16)
        prob_grad = jnp.einsum(
            "rqhe,rkhe->rhqk", up_block, value_chosen, preferred_element_type=jnp.float32
        )
        row_delta = jnp.sum(prob_full * prob_grad, axis=-1, keepdims=True)
        score_grad = (prob_full * (prob_grad - row_delta) * score_scale).astype(jnp.bfloat16)
        query_grad = jnp.einsum(
            "rhqk,rkhe->rqhe", score_grad, key_chosen, preferred_element_type=jnp.float32
        ).astype(jnp.bfloat16)
        key_terms = jnp.einsum(
            "rhqk,rqhe->rkhe", score_grad, query_block, preferred_element_type=jnp.float32
        )
        value_terms = jnp.einsum(
            "rhqk,rqhe->rkhe", prob_low, up_block, preferred_element_type=jnp.float32
        )
        key_grad = key_grad.at[slot_block].add(
            key_terms.reshape(group_size, NBK, BLOCK, heads_here, HEAD)
        )
        value_grad = value_grad.at[slot_block].add(
            value_terms.reshape(group_size, NBK, BLOCK, heads_here, HEAD)
        )
        return ((key_grad, value_grad), (out_block, query_grad))

    zero_start = jnp.zeros((zero_count * local_blocks, BLOCK, heads_here, HEAD), jnp.float32)
    (key_grad, value_grad), (out_blocks, query_grads) = lax.scan(
        attend, (zero_start, zero_start), (queries, incoming, key_slots)
    )
    attended = lax.all_to_all(
        out_blocks.reshape(local_blocks * BLOCK, 1, head_cols),
        "seq",
        split_axis=0,
        concat_axis=1,
        tiled=True,
    )
    attended = attended.reshape(tok_rows, seq_count * head_cols)
    key_sum, value_sum = (
        lax.psum_scatter(
            key_grad.astype(jnp.bfloat16), "zero", scatter_dimension=0, tiled=True
        ).astype(jnp.float32),
        lax.psum_scatter(
            value_grad.astype(jnp.bfloat16), "zero", scatter_dimension=0, tiled=True
        ).astype(jnp.float32),
    )
    local_grads = jnp.stack(
        [
            query_grads.reshape(-1, head_cols),
            key_sum.astype(jnp.bfloat16).reshape(-1, head_cols),
            value_sum.astype(jnp.bfloat16).reshape(-1, head_cols),
        ],
        axis=1,
    )
    local_grads = local_grads.reshape(local_blocks * BLOCK, 3, 1, head_cols)
    token_grads = lax.all_to_all(local_grads, "seq", split_axis=0, concat_axis=2, tiled=True)
    flat_grads = token_grads.reshape(tok_rows, 3 * seq_count * head_cols)
    token_gradient = jnp.einsum(
        "tc,dc->td", flat_grads, weights, preferred_element_type=jnp.float32
    ).astype(jnp.bfloat16)
    group_tokens = lax.all_gather(tokens, "seq", axis=0, tiled=True)
    head_grads = local_grads.reshape(local_blocks * BLOCK, 3 * head_cols)
    head_part = jnp.einsum(
        "td,tc->dc", group_tokens, head_grads, preferred_element_type=jnp.float32
    )
    own_rows = lax.psum_scatter(head_part, "zero", scatter_dimension=0, tiled=True)
    own_rows = own_rows.reshape(1, -1, 3, head_cols)
    gathered = lax.all_gather(own_rows, "seq", axis=0, tiled=True)
    weight_gradient = gathered.transpose(1, 2, 0, 3).reshape(-1, 3 * seq_count * head_cols)
    return (attended, token_gradient, weight_gradient)


def solution(mesh):
    return jax.shard_map(
        on_device,
        mesh=mesh,
        in_specs=(P(("seq", "zero"), None), P("zero", None), P(), P(("seq", "zero"), None)),
        out_specs=(P(("seq", "zero"), None), P(("seq", "zero"), None), P("zero", None)),
        check_vma=False,
    )
```

```python
import jax
import jax.numpy as jnp
from jax import lax
from jax.sharding import PartitionSpec as P

HEADS = 16
HEAD = 64
BLOCK = 128
NBK = 8


def on_device(tokens, projection, pattern, upstream):
    seq_count = lax.axis_size("seq")
    zero_count = lax.axis_size("zero")
    zero_index = lax.axis_index("zero")
    tok_rows = tokens.shape[0]
    model_width = tokens.shape[1]
    heads_here = HEADS // seq_count
    head_cols = heads_here * HEAD
    per_shard = tok_rows // BLOCK
    local_blocks = seq_count * per_shard
    group_size = 4
    step_count = local_blocks // group_size
    score_scale = HEAD ** (-0.5)
    seq_index = lax.axis_index("seq")
    weights = lax.all_gather(projection, "zero", axis=0, tiled=True)
    group_tokens = lax.all_gather(tokens, "seq", axis=0, tiled=True)
    head_w = projection.reshape(projection.shape[0], 3, seq_count, head_cols)
    head_w = lax.dynamic_index_in_dim(head_w, seq_index, axis=2, keepdims=False)
    head_w = lax.all_gather(head_w, "zero", axis=0, tiled=True)
    by_head = jnp.einsum(
        "td,dgc->tgc", group_tokens, head_w, preferred_element_type=jnp.float32
    ).astype(jnp.bfloat16)
    kv_all = lax.all_gather(by_head[:, 1:], "zero", axis=0, tiled=True)
    key_all = kv_all[:, 0].reshape(zero_count * local_blocks, BLOCK, heads_here, HEAD)
    value_all = kv_all[:, 1].reshape(zero_count * local_blocks, BLOCK, heads_here, HEAD)
    queries = by_head[:, 0].reshape(step_count, group_size, BLOCK, heads_here, HEAD)
    incoming = lax.all_to_all(
        upstream.reshape(tok_rows, seq_count, head_cols),
        "seq",
        split_axis=1,
        concat_axis=0,
        tiled=True,
    )
    incoming = incoming.reshape(step_count, group_size, BLOCK, heads_here, HEAD)
    local_ids = jnp.arange(local_blocks, dtype=jnp.int32)
    row_ids = (local_ids // per_shard * zero_count + zero_index) * per_shard + local_ids % per_shard
    row_lists = pattern[row_ids]
    shard_ids = row_lists // per_shard
    key_slots = (
        shard_ids % zero_count * local_blocks
        + shard_ids // zero_count * per_shard
        + row_lists % per_shard
    )
    key_slots = key_slots.reshape(step_count, group_size, NBK)

    def attend(carried, inputs):
        key_grad, value_grad = carried
        query_block, up_block, slot_block = inputs
        key_chosen = key_all[slot_block].reshape(group_size, NBK * BLOCK, heads_here, HEAD)
        value_chosen = value_all[slot_block].reshape(group_size, NBK * BLOCK, heads_here, HEAD)
        scores = (
            jnp.einsum(
                "rqhe,rkhe->rhqk", query_block, key_chosen, preferred_element_type=jnp.float32
            )
            * score_scale
        )
        row_max = jnp.max(scores, axis=-1, keepdims=True)
        exponent = jnp.exp(scores - row_max)
        prob_full = exponent / jnp.sum(exponent, axis=-1, keepdims=True)
        prob_low = prob_full.astype(jnp.bfloat16)
        out_block = jnp.einsum(
            "rhqk,rkhe->rqhe", prob_low, value_chosen, preferred_element_type=jnp.float32
        ).astype(jnp.bfloat16)
        prob_grad = jnp.einsum(
            "rqhe,rkhe->rhqk", up_block, value_chosen, preferred_element_type=jnp.float32
        )
        row_delta = jnp.sum(prob_full * prob_grad, axis=-1, keepdims=True)
        score_grad = (prob_full * (prob_grad - row_delta) * score_scale).astype(jnp.bfloat16)
        query_grad = jnp.einsum(
            "rhqk,rkhe->rqhe", score_grad, key_chosen, preferred_element_type=jnp.float32
        ).astype(jnp.bfloat16)
        key_terms = jnp.einsum(
            "rhqk,rqhe->rkhe", score_grad, query_block, preferred_element_type=jnp.float32
        )
        value_terms = jnp.einsum(
            "rhqk,rqhe->rkhe", prob_low, up_block, preferred_element_type=jnp.float32
        )
        key_grad = key_grad.at[slot_block].add(
            key_terms.reshape(group_size, NBK, BLOCK, heads_here, HEAD)
        )
        value_grad = value_grad.at[slot_block].add(
            value_terms.reshape(group_size, NBK, BLOCK, heads_here, HEAD)
        )
        return ((key_grad, value_grad), (out_block, query_grad))

    zero_start = jnp.zeros((zero_count * local_blocks, BLOCK, heads_here, HEAD), jnp.float32)
    half = step_count // 2
    carried, (out_a, query_a) = lax.scan(
        attend,
        (zero_start, zero_start),
        (queries[:half], incoming[:half], key_slots[:half]),
    )
    weights, carried = lax.optimization_barrier((weights, carried))
    (key_grad, value_grad), (out_b, query_b) = lax.scan(
        attend, carried, (queries[half:], incoming[half:], key_slots[half:])
    )
    out_blocks = jnp.concatenate([out_a, out_b], axis=0)
    query_grads = jnp.concatenate([query_a, query_b], axis=0)
    attended = lax.all_to_all(
        out_blocks.reshape(local_blocks * BLOCK, 1, head_cols),
        "seq",
        split_axis=0,
        concat_axis=1,
        tiled=True,
    )
    attended = attended.reshape(tok_rows, seq_count * head_cols)
    key_sum, value_sum = (
        lax.psum_scatter(
            key_grad.astype(jnp.bfloat16), "zero", scatter_dimension=0, tiled=True
        ).astype(jnp.float32),
        lax.psum_scatter(
            value_grad.astype(jnp.bfloat16), "zero", scatter_dimension=0, tiled=True
        ).astype(jnp.float32),
    )
    local_grads = jnp.stack(
        [
            query_grads.reshape(-1, head_cols),
            key_sum.astype(jnp.bfloat16).reshape(-1, head_cols),
            value_sum.astype(jnp.bfloat16).reshape(-1, head_cols),
        ],
        axis=1,
    )
    local_grads = local_grads.reshape(local_blocks * BLOCK, 3, 1, head_cols)
    token_grads = lax.all_to_all(local_grads, "seq", split_axis=0, concat_axis=2, tiled=True)
    flat_grads = token_grads.reshape(tok_rows, 3 * seq_count * head_cols)
    token_gradient = jnp.einsum(
        "tc,dc->td", flat_grads, weights, preferred_element_type=jnp.float32
    ).astype(jnp.bfloat16)
    head_grads = local_grads.reshape(local_blocks * BLOCK, 3 * head_cols)
    head_part = jnp.einsum(
        "td,tc->dc", group_tokens, head_grads, preferred_element_type=jnp.float32
    )
    own_rows = lax.psum_scatter(head_part, "zero", scatter_dimension=0, tiled=True)
    own_rows = own_rows.reshape(1, -1, 3, head_cols)
    gathered = lax.all_gather(own_rows, "seq", axis=0, tiled=True)
    weight_gradient = gathered.transpose(1, 2, 0, 3).reshape(-1, 3 * seq_count * head_cols)
    return (attended, token_gradient, weight_gradient)


def solution(mesh):
    return jax.shard_map(
        on_device,
        mesh=mesh,
        in_specs=(P(("seq", "zero"), None), P("zero", None), P(), P(("seq", "zero"), None)),
        out_specs=(P(("seq", "zero"), None), P(("seq", "zero"), None), P("zero", None)),
        check_vma=False,
    )
```

```python
import jax
import jax.numpy as jnp
from jax import lax
from jax.sharding import PartitionSpec as P

HEADS = 16
HEAD = 64
BLOCK = 128
NBK = 8


def on_device(tokens, projection, pattern, upstream):
    seq_count = lax.axis_size("seq")
    zero_count = lax.axis_size("zero")
    zero_index = lax.axis_index("zero")
    tok_rows = tokens.shape[0]
    model_width = tokens.shape[1]
    heads_here = HEADS // seq_count
    head_cols = heads_here * HEAD
    per_shard = tok_rows // BLOCK
    local_blocks = seq_count * per_shard
    group_size = 4
    step_count = local_blocks // group_size
    score_scale = HEAD ** (-0.5)
    seq_index = lax.axis_index("seq")
    weights = lax.all_gather(projection, "zero", axis=0, tiled=True)
    group_tokens = lax.all_gather(tokens, "seq", axis=0, tiled=True)
    head_w = projection.reshape(projection.shape[0], 3, seq_count, head_cols)
    head_w = lax.dynamic_index_in_dim(head_w, seq_index, axis=2, keepdims=False)
    head_w = lax.all_gather(head_w, "zero", axis=0, tiled=True)
    by_head = jnp.einsum(
        "td,dgc->tgc", group_tokens, head_w, preferred_element_type=jnp.float32
    ).astype(jnp.bfloat16)
    kv_all = lax.all_gather(by_head[:, 1:], "zero", axis=0, tiled=True)
    key_all = kv_all[:, 0].reshape(zero_count * local_blocks, BLOCK, heads_here, HEAD)
    value_all = kv_all[:, 1].reshape(zero_count * local_blocks, BLOCK, heads_here, HEAD)
    queries = by_head[:, 0].reshape(step_count, group_size, BLOCK, heads_here, HEAD)
    incoming = lax.all_to_all(
        upstream.reshape(tok_rows, seq_count, head_cols),
        "seq",
        split_axis=1,
        concat_axis=0,
        tiled=True,
    )
    incoming = incoming.reshape(step_count, group_size, BLOCK, heads_here, HEAD)
    local_ids = jnp.arange(local_blocks, dtype=jnp.int32)
    row_ids = (local_ids // per_shard * zero_count + zero_index) * per_shard + local_ids % per_shard
    row_lists = pattern[row_ids]
    shard_ids = row_lists // per_shard
    key_slots = (
        shard_ids % zero_count * local_blocks
        + shard_ids // zero_count * per_shard
        + row_lists % per_shard
    )
    key_slots = key_slots.reshape(step_count, group_size, NBK)

    def attend(carried, inputs):
        key_grad, value_grad = carried
        query_block, up_block, slot_block = inputs
        key_chosen = key_all[slot_block].reshape(group_size, NBK * BLOCK, heads_here, HEAD)
        value_chosen = value_all[slot_block].reshape(group_size, NBK * BLOCK, heads_here, HEAD)
        scores = (
            jnp.einsum(
                "rqhe,rkhe->rhqk", query_block, key_chosen, preferred_element_type=jnp.float32
            )
            * score_scale
        )
        row_max = jnp.max(scores, axis=-1, keepdims=True)
        exponent = jnp.exp(scores - row_max)
        prob_full = exponent / jnp.sum(exponent, axis=-1, keepdims=True)
        prob_low = prob_full.astype(jnp.bfloat16)
        out_block = jnp.einsum(
            "rhqk,rkhe->rqhe", prob_low, value_chosen, preferred_element_type=jnp.float32
        ).astype(jnp.bfloat16)
        prob_grad = jnp.einsum(
            "rqhe,rkhe->rhqk", up_block, value_chosen, preferred_element_type=jnp.float32
        )
        row_delta = jnp.sum(prob_full * prob_grad, axis=-1, keepdims=True)
        score_grad = (prob_full * (prob_grad - row_delta) * score_scale).astype(jnp.bfloat16)
        query_grad = jnp.einsum(
            "rhqk,rkhe->rqhe", score_grad, key_chosen, preferred_element_type=jnp.float32
        ).astype(jnp.bfloat16)
        key_terms = jnp.einsum(
            "rhqk,rqhe->rkhe", score_grad, query_block, preferred_element_type=jnp.float32
        )
        value_terms = jnp.einsum(
            "rhqk,rqhe->rkhe", prob_low, up_block, preferred_element_type=jnp.float32
        )
        key_grad = key_grad.at[slot_block].add(
            key_terms.reshape(group_size, NBK, BLOCK, heads_here, HEAD)
        )
        value_grad = value_grad.at[slot_block].add(
            value_terms.reshape(group_size, NBK, BLOCK, heads_here, HEAD)
        )
        return ((key_grad, value_grad), (out_block, query_grad))

    zero_start = jnp.zeros((zero_count * local_blocks, BLOCK, heads_here, HEAD), jnp.float32)
    half = step_count // 2
    carried, (out_a, query_a) = lax.scan(
        attend,
        (zero_start, zero_start),
        (queries[:half], incoming[:half], key_slots[:half]),
    )
    weights, carried = lax.optimization_barrier((weights, carried))
    (key_grad, value_grad), (out_b, query_b) = lax.scan(
        attend, carried, (queries[half:], incoming[half:], key_slots[half:])
    )
    out_blocks = jnp.concatenate([out_a, out_b], axis=0)
    query_grads = jnp.concatenate([query_a, query_b], axis=0)
    attended = lax.all_to_all(
        out_blocks.reshape(local_blocks * BLOCK, 1, head_cols),
        "seq",
        split_axis=0,
        concat_axis=1,
        tiled=True,
    )
    attended = attended.reshape(tok_rows, seq_count * head_cols)
    group_sums = jnp.stack([key_grad, value_grad], axis=1).astype(jnp.bfloat16)
    group_sums = group_sums.reshape(zero_count, local_blocks, 2, BLOCK, head_cols)
    group_sums = lax.all_to_all(group_sums, "zero", split_axis=0, concat_axis=0, tiled=True)
    kv_sum = jnp.sum(group_sums.astype(jnp.float32), axis=0)
    key_sum, value_sum = kv_sum[:, 0], kv_sum[:, 1]
    local_grads = jnp.stack(
        [
            query_grads.reshape(-1, head_cols),
            key_sum.astype(jnp.bfloat16).reshape(-1, head_cols),
            value_sum.astype(jnp.bfloat16).reshape(-1, head_cols),
        ],
        axis=1,
    )
    local_grads = local_grads.reshape(local_blocks * BLOCK, 3, 1, head_cols)
    token_grads = lax.all_to_all(local_grads, "seq", split_axis=0, concat_axis=2, tiled=True)
    flat_grads = token_grads.reshape(tok_rows, 3 * seq_count * head_cols)
    token_gradient = jnp.einsum(
        "tc,dc->td", flat_grads, weights, preferred_element_type=jnp.float32
    ).astype(jnp.bfloat16)
    head_grads = local_grads.reshape(local_blocks * BLOCK, 3 * head_cols)
    head_part = jnp.einsum(
        "td,tc->dc", group_tokens, head_grads, preferred_element_type=jnp.float32
    )
    head_part = head_part.reshape(zero_count, -1, 3 * head_cols)
    head_part = lax.all_to_all(head_part, "zero", split_axis=0, concat_axis=0, tiled=True)
    own_rows = jnp.sum(head_part, axis=0)
    own_rows = own_rows.reshape(1, -1, 3, head_cols)
    gathered = lax.all_gather(own_rows, "seq", axis=0, tiled=True)
    weight_gradient = gathered.transpose(1, 2, 0, 3).reshape(-1, 3 * seq_count * head_cols)
    return (attended, token_gradient, weight_gradient)


def solution(mesh):
    return jax.shard_map(
        on_device,
        mesh=mesh,
        in_specs=(P(("seq", "zero"), None), P("zero", None), P(), P(("seq", "zero"), None)),
        out_specs=(P(("seq", "zero"), None), P(("seq", "zero"), None), P("zero", None)),
        check_vma=False,
    )
```

```python
import functools
import jax
import jax.numpy as jnp
from jax import lax
from jax.sharding import PartitionSpec as P
from jax.experimental import pallas as pl
from jax.experimental.pallas import tpu as pltpu

HEADS = 16
HEAD = 64
BLOCK = 128
NBK = 8


def _attn_kernel(slots_ref, q_ref, up_ref, k_ref, v_ref, out_ref, qg_ref, kg_ref, vg_ref, *, scale):
    i = pl.program_id(0)

    @pl.when(i == 0)
    def _():
        kg_ref[...] = jnp.zeros(kg_ref.shape, kg_ref.dtype)
        vg_ref[...] = jnp.zeros(vg_ref.shape, vg_ref.dtype)

    q = q_ref[0]
    up = up_ref[0]
    ids = [slots_ref[i, j] for j in range(NBK)]
    keys = jnp.concatenate([k_ref[ids[j]] for j in range(NBK)], axis=0)
    vals = jnp.concatenate([v_ref[ids[j]] for j in range(NBK)], axis=0)
    nt = (((1,), (1,)), ((), ()))
    tn = (((0,), (0,)), ((), ()))
    scores = lax.dot_general(q, keys, nt, preferred_element_type=jnp.float32) * scale
    row_max = jnp.max(scores, axis=-1, keepdims=True)
    exponent = jnp.exp(scores - row_max)
    prob_full = exponent / jnp.sum(exponent, axis=-1, keepdims=True)
    prob_low = prob_full.astype(jnp.bfloat16)
    out_ref[0] = jnp.dot(prob_low, vals, preferred_element_type=jnp.float32).astype(out_ref.dtype)
    prob_grad = lax.dot_general(up, vals, nt, preferred_element_type=jnp.float32)
    row_delta = jnp.sum(prob_full * prob_grad, axis=-1, keepdims=True)
    score_grad = (prob_full * (prob_grad - row_delta) * scale).astype(jnp.bfloat16)
    qg_ref[0] = jnp.dot(score_grad, keys, preferred_element_type=jnp.float32).astype(qg_ref.dtype)
    key_terms = lax.dot_general(score_grad, q, tn, preferred_element_type=jnp.float32)
    value_terms = lax.dot_general(prob_low, up, tn, preferred_element_type=jnp.float32)
    for j in range(NBK):
        kg_ref[ids[j]] += key_terms[j * BLOCK:(j + 1) * BLOCK]
        vg_ref[ids[j]] += value_terms[j * BLOCK:(j + 1) * BLOCK]


def block_attention(slots, queries, upstream, keys, values, scale):
    rows = queries.shape[0]
    slot_count = keys.shape[0]
    row_spec = pl.BlockSpec((1, BLOCK, HEAD), lambda i, s: (i, 0, 0))
    full_spec = pl.BlockSpec((slot_count, BLOCK, HEAD), lambda i, s: (0, 0, 0))
    grid_spec = pltpu.PrefetchScalarGridSpec(
        num_scalar_prefetch=1,
        grid=(rows,),
        in_specs=[row_spec, row_spec, full_spec, full_spec],
        out_specs=[row_spec, row_spec, full_spec, full_spec],
    )
    out_shape = [
        jax.ShapeDtypeStruct((rows, BLOCK, HEAD), jnp.bfloat16),
        jax.ShapeDtypeStruct((rows, BLOCK, HEAD), jnp.bfloat16),
        jax.ShapeDtypeStruct((slot_count, BLOCK, HEAD), jnp.float32),
        jax.ShapeDtypeStruct((slot_count, BLOCK, HEAD), jnp.float32),
    ]
    return pl.pallas_call(
        functools.partial(_attn_kernel, scale=scale),
        grid_spec=grid_spec,
        out_shape=out_shape,
        compiler_params=pltpu.CompilerParams(dimension_semantics=("arbitrary",), vmem_limit_bytes=48 * 1024 * 1024),
    )(slots, queries, upstream, keys, values)


def on_device(tokens, projection, pattern, upstream):
    seq_count = lax.axis_size("seq")
    zero_count = lax.axis_size("zero")
    zero_index = lax.axis_index("zero")
    tok_rows = tokens.shape[0]
    model_width = tokens.shape[1]
    heads_here = HEADS // seq_count
    head_cols = heads_here * HEAD
    per_shard = tok_rows // BLOCK
    local_blocks = seq_count * per_shard
    group_size = 4
    step_count = local_blocks // group_size
    score_scale = HEAD ** (-0.5)
    seq_index = lax.axis_index("seq")
    weights = lax.all_gather(projection, "zero", axis=0, tiled=True)
    group_tokens = lax.all_gather(tokens, "seq", axis=0, tiled=True)
    head_w = projection.reshape(projection.shape[0], 3, seq_count, head_cols)
    head_w = lax.dynamic_index_in_dim(head_w, seq_index, axis=2, keepdims=False)
    head_w = lax.all_gather(head_w, "zero", axis=0, tiled=True)
    by_head = jnp.einsum(
        "td,dgc->tgc", group_tokens, head_w, preferred_element_type=jnp.float32
    ).astype(jnp.bfloat16)
    kv_all = lax.all_gather(by_head[:, 1:], "zero", axis=0, tiled=True)
    key_all = kv_all[:, 0].reshape(zero_count * local_blocks, BLOCK, heads_here, HEAD)
    value_all = kv_all[:, 1].reshape(zero_count * local_blocks, BLOCK, heads_here, HEAD)
    queries = by_head[:, 0].reshape(step_count, group_size, BLOCK, heads_here, HEAD)
    incoming = lax.all_to_all(
        upstream.reshape(tok_rows, seq_count, head_cols),
        "seq",
        split_axis=1,
        concat_axis=0,
        tiled=True,
    )
    incoming = incoming.reshape(step_count, group_size, BLOCK, heads_here, HEAD)
    local_ids = jnp.arange(local_blocks, dtype=jnp.int32)
    row_ids = (local_ids // per_shard * zero_count + zero_index) * per_shard + local_ids % per_shard
    row_lists = pattern[row_ids]
    shard_ids = row_lists // per_shard
    key_slots = (
        shard_ids % zero_count * local_blocks
        + shard_ids // zero_count * per_shard
        + row_lists % per_shard
    )
    key_slots = key_slots.reshape(step_count, group_size, NBK)

    out_blocks, query_grads, key_grad, value_grad = block_attention(
        key_slots.reshape(local_blocks, NBK),
        queries.reshape(local_blocks, BLOCK, head_cols),
        incoming.reshape(local_blocks, BLOCK, head_cols),
        key_all.reshape(-1, BLOCK, head_cols),
        value_all.reshape(-1, BLOCK, head_cols),
        score_scale,
    )
    attended = lax.all_to_all(
        out_blocks.reshape(local_blocks * BLOCK, 1, head_cols),
        "seq",
        split_axis=0,
        concat_axis=1,
        tiled=True,
    )
    attended = attended.reshape(tok_rows, seq_count * head_cols)
    group_sums = jnp.stack([key_grad, value_grad], axis=1).astype(jnp.bfloat16)
    group_sums = group_sums.reshape(zero_count, local_blocks, 2, BLOCK, head_cols)
    group_sums = lax.all_to_all(group_sums, "zero", split_axis=0, concat_axis=0, tiled=True)
    kv_sum = jnp.sum(group_sums.astype(jnp.float32), axis=0)
    key_sum, value_sum = kv_sum[:, 0], kv_sum[:, 1]
    local_grads = jnp.stack(
        [
            query_grads.reshape(-1, head_cols),
            key_sum.astype(jnp.bfloat16).reshape(-1, head_cols),
            value_sum.astype(jnp.bfloat16).reshape(-1, head_cols),
        ],
        axis=1,
    )
    local_grads = local_grads.reshape(local_blocks * BLOCK, 3, 1, head_cols)
    token_grads = lax.all_to_all(local_grads, "seq", split_axis=0, concat_axis=2, tiled=True)
    flat_grads = token_grads.reshape(tok_rows, 3 * seq_count * head_cols)
    token_gradient = jnp.einsum(
        "tc,dc->td", flat_grads, weights, preferred_element_type=jnp.float32
    ).astype(jnp.bfloat16)
    head_grads = local_grads.reshape(local_blocks * BLOCK, 3 * head_cols)
    head_part = jnp.einsum(
        "td,tc->dc", group_tokens, head_grads, preferred_element_type=jnp.float32
    )
    head_part = head_part.reshape(zero_count, -1, 3 * head_cols)
    head_part = lax.all_to_all(head_part, "zero", split_axis=0, concat_axis=0, tiled=True)
    own_rows = jnp.sum(head_part, axis=0)
    own_rows = own_rows.reshape(1, -1, 3, head_cols)
    gathered = lax.all_gather(own_rows, "seq", axis=0, tiled=True)
    weight_gradient = gathered.transpose(1, 2, 0, 3).reshape(-1, 3 * seq_count * head_cols)
    return (attended, token_gradient, weight_gradient)


def solution(mesh):
    return jax.shard_map(
        on_device,
        mesh=mesh,
        in_specs=(P(("seq", "zero"), None), P("zero", None), P(), P(("seq", "zero"), None)),
        out_specs=(P(("seq", "zero"), None), P(("seq", "zero"), None), P("zero", None)),
        check_vma=False,
    )
```

```python
import functools
import jax
import jax.numpy as jnp
from jax import lax
from jax.sharding import PartitionSpec as P
from jax.experimental import pallas as pl
from jax.experimental.pallas import tpu as pltpu

HEADS = 16
HEAD = 64
BLOCK = 128
NBK = 8


def _attn_kernel(slots_ref, q_ref, up_ref, kv_ref, out_ref, qg_ref, kvg_ref, acc_ref, *, scale):
    i = pl.program_id(0)

    @pl.when(i == 0)
    def _():
        acc_ref[...] = jnp.zeros(acc_ref.shape, acc_ref.dtype)

    q = q_ref[0]
    up = up_ref[0]
    ids = [slots_ref[i, j] for j in range(NBK)]
    blocks = [kv_ref[ids[j]] for j in range(NBK)]
    keys = jnp.concatenate([b[:, :HEAD] for b in blocks], axis=0)
    vals = jnp.concatenate([b[:, HEAD:] for b in blocks], axis=0)
    nt = (((1,), (1,)), ((), ()))
    tn = (((0,), (0,)), ((), ()))
    scores = lax.dot_general(q, keys, nt, preferred_element_type=jnp.float32) * scale
    row_max = jnp.max(scores, axis=-1, keepdims=True)
    exponent = jnp.exp(scores - row_max)
    prob_full = exponent / jnp.sum(exponent, axis=-1, keepdims=True)
    prob_low = prob_full.astype(jnp.bfloat16)
    out_ref[0] = jnp.dot(prob_low, vals, preferred_element_type=jnp.float32).astype(out_ref.dtype)
    prob_grad = lax.dot_general(up, vals, nt, preferred_element_type=jnp.float32)
    row_delta = jnp.sum(prob_full * prob_grad, axis=-1, keepdims=True)
    score_grad = (prob_full * (prob_grad - row_delta) * scale).astype(jnp.bfloat16)
    qg_ref[0] = jnp.dot(score_grad, keys, preferred_element_type=jnp.float32).astype(qg_ref.dtype)
    key_terms = lax.dot_general(score_grad, q, tn, preferred_element_type=jnp.float32)
    value_terms = lax.dot_general(prob_low, up, tn, preferred_element_type=jnp.float32)
    terms = jnp.concatenate([key_terms, value_terms], axis=1)
    for j in range(NBK):
        acc_ref[ids[j]] += terms[j * BLOCK:(j + 1) * BLOCK]

    @pl.when(i == pl.num_programs(0) - 1)
    def _():
        kvg_ref[...] = acc_ref[...].astype(kvg_ref.dtype)


def block_attention(slots, queries, upstream, kv, scale):
    rows = queries.shape[0]
    slot_count = kv.shape[0]
    row_spec = pl.BlockSpec((1, BLOCK, HEAD), lambda i, s: (i, 0, 0))
    full_spec = pl.BlockSpec((slot_count, BLOCK, 2 * HEAD), lambda i, s: (0, 0, 0))
    grid_spec = pltpu.PrefetchScalarGridSpec(
        num_scalar_prefetch=1,
        grid=(rows,),
        in_specs=[row_spec, row_spec, full_spec],
        out_specs=[row_spec, row_spec, full_spec],
        scratch_shapes=[pltpu.VMEM((slot_count, BLOCK, 2 * HEAD), jnp.float32)],
    )
    out_shape = [
        jax.ShapeDtypeStruct((rows, BLOCK, HEAD), jnp.bfloat16),
        jax.ShapeDtypeStruct((rows, BLOCK, HEAD), jnp.bfloat16),
        jax.ShapeDtypeStruct((slot_count, BLOCK, 2 * HEAD), jnp.bfloat16),
    ]
    return pl.pallas_call(
        functools.partial(_attn_kernel, scale=scale),
        grid_spec=grid_spec,
        out_shape=out_shape,
        compiler_params=pltpu.CompilerParams(
            dimension_semantics=("arbitrary",), vmem_limit_bytes=48 * 1024 * 1024
        ),
    )(slots, queries, upstream, kv)


def on_device(tokens, projection, pattern, upstream):
    seq_count = lax.axis_size("seq")
    zero_count = lax.axis_size("zero")
    zero_index = lax.axis_index("zero")
    tok_rows = tokens.shape[0]
    model_width = tokens.shape[1]
    heads_here = HEADS // seq_count
    head_cols = heads_here * HEAD
    per_shard = tok_rows // BLOCK
    local_blocks = seq_count * per_shard
    score_scale = HEAD ** (-0.5)
    seq_index = lax.axis_index("seq")
    weights = lax.all_gather(projection, "zero", axis=0, tiled=True)
    group_tokens = lax.all_gather(tokens, "seq", axis=0, tiled=True)
    head_w = projection.reshape(projection.shape[0], 3, seq_count, head_cols)
    head_w = lax.dynamic_index_in_dim(head_w, seq_index, axis=2, keepdims=False)
    head_w = lax.all_gather(head_w, "zero", axis=0, tiled=True)
    queries = jnp.einsum(
        "td,dc->tc", group_tokens, head_w[:, 0], preferred_element_type=jnp.float32
    ).astype(jnp.bfloat16)
    kv_local = jnp.einsum(
        "td,dc->tc",
        group_tokens,
        head_w[:, 1:].reshape(-1, 2 * head_cols),
        preferred_element_type=jnp.float32,
    ).astype(jnp.bfloat16)
    kv_all = lax.all_gather(kv_local, "zero", axis=0, tiled=True)
    incoming = lax.all_to_all(
        upstream.reshape(tok_rows, seq_count, head_cols),
        "seq",
        split_axis=1,
        concat_axis=0,
        tiled=True,
    )
    local_ids = jnp.arange(local_blocks, dtype=jnp.int32)
    row_ids = (local_ids // per_shard * zero_count + zero_index) * per_shard + local_ids % per_shard
    row_lists = pattern[row_ids]
    shard_ids = row_lists // per_shard
    key_slots = (
        shard_ids % zero_count * local_blocks
        + shard_ids // zero_count * per_shard
        + row_lists % per_shard
    )

    out_blocks, query_grads, group_sums = block_attention(
        key_slots.reshape(local_blocks, NBK),
        queries.reshape(local_blocks, BLOCK, head_cols),
        incoming.reshape(local_blocks, BLOCK, head_cols),
        kv_all.reshape(-1, BLOCK, 2 * head_cols),
        score_scale,
    )
    attended = lax.all_to_all(
        out_blocks.reshape(local_blocks * BLOCK, 1, head_cols),
        "seq",
        split_axis=0,
        concat_axis=1,
        tiled=True,
    )
    attended = attended.reshape(tok_rows, seq_count * head_cols)
    group_sums = group_sums.reshape(zero_count, local_blocks * BLOCK, 2 * head_cols)
    group_sums = lax.all_to_all(group_sums, "zero", split_axis=0, concat_axis=0, tiled=True)
    kv_sum = jnp.sum(group_sums.astype(jnp.float32), axis=0).astype(jnp.bfloat16)
    local_grads = jnp.concatenate([query_grads.reshape(-1, head_cols), kv_sum], axis=1)
    local_grads = local_grads.reshape(local_blocks * BLOCK, 3, 1, head_cols)
    token_grads = lax.all_to_all(local_grads, "seq", split_axis=0, concat_axis=2, tiled=True)
    flat_grads = token_grads.reshape(tok_rows, 3 * seq_count * head_cols)
    token_gradient = jnp.einsum(
        "tc,dc->td", flat_grads, weights, preferred_element_type=jnp.float32
    ).astype(jnp.bfloat16)
    head_grads = local_grads.reshape(local_blocks * BLOCK, 3 * head_cols)
    head_part = jnp.einsum(
        "td,tc->dc", group_tokens, head_grads, preferred_element_type=jnp.float32
    )
    head_part = head_part.reshape(zero_count, -1, 3 * head_cols)
    head_part = lax.all_to_all(head_part, "zero", split_axis=0, concat_axis=0, tiled=True)
    own_rows = jnp.sum(head_part, axis=0)
    own_rows = own_rows.reshape(1, -1, 3, head_cols)
    gathered = lax.all_gather(own_rows, "seq", axis=0, tiled=True)
    weight_gradient = gathered.transpose(1, 2, 0, 3).reshape(-1, 3 * seq_count * head_cols)
    return (attended, token_gradient, weight_gradient)


def solution(mesh):
    return jax.shard_map(
        on_device,
        mesh=mesh,
        in_specs=(P(("seq", "zero"), None), P("zero", None), P(), P(("seq", "zero"), None)),
        out_specs=(P(("seq", "zero"), None), P(("seq", "zero"), None), P("zero", None)),
        check_vma=False,
    )
```

```python
import functools
import jax
import jax.numpy as jnp
from jax import lax
from jax.sharding import PartitionSpec as P
from jax.experimental import pallas as pl
from jax.experimental.pallas import tpu as pltpu

HEADS = 16
HEAD = 64
BLOCK = 128
NBK = 8


def _attn_kernel(slots_ref, q_ref, up_ref, kv_ref, out_ref, qg_ref, kvg_ref, acc_ref, *, scale):
    i = pl.program_id(0)

    @pl.when(i == 0)
    def _():
        acc_ref[...] = jnp.zeros(acc_ref.shape, acc_ref.dtype)

    q = q_ref[0]
    up = up_ref[0]
    ids = [slots_ref[i, j] for j in range(NBK)]
    blocks = [kv_ref[ids[j]] for j in range(NBK)]
    keys = jnp.concatenate([b[:, :HEAD] for b in blocks], axis=0)
    vals = jnp.concatenate([b[:, HEAD:] for b in blocks], axis=0)
    nt = (((1,), (1,)), ((), ()))
    tn = (((0,), (0,)), ((), ()))
    scores = lax.dot_general(q, keys, nt, preferred_element_type=jnp.float32) * scale
    row_max = jnp.max(scores, axis=-1, keepdims=True)
    exponent = jnp.exp(scores - row_max)
    prob_full = exponent / jnp.sum(exponent, axis=-1, keepdims=True)
    prob_low = prob_full.astype(jnp.bfloat16)
    out_ref[0] = jnp.dot(prob_low, vals, preferred_element_type=jnp.float32).astype(out_ref.dtype)
    prob_grad = lax.dot_general(up, vals, nt, preferred_element_type=jnp.float32)
    row_delta = jnp.sum(prob_full * prob_grad, axis=-1, keepdims=True)
    score_grad = (prob_full * (prob_grad - row_delta) * scale).astype(jnp.bfloat16)
    qg_ref[0] = jnp.dot(score_grad, keys, preferred_element_type=jnp.float32).astype(qg_ref.dtype)
    key_terms = lax.dot_general(score_grad, q, tn, preferred_element_type=jnp.float32)
    value_terms = lax.dot_general(prob_low, up, tn, preferred_element_type=jnp.float32)
    terms = jnp.concatenate([key_terms, value_terms], axis=1)
    for j in range(NBK):
        acc_ref[ids[j]] += terms[j * BLOCK:(j + 1) * BLOCK]

    @pl.when(i == pl.num_programs(0) - 1)
    def _():
        kvg_ref[...] = acc_ref[...].astype(kvg_ref.dtype)


def block_attention(slots, queries, upstream, kv, scale):
    rows = queries.shape[0]
    slot_count = kv.shape[0]
    row_spec = pl.BlockSpec((1, BLOCK, HEAD), lambda i, s: (i, 0, 0))
    full_spec = pl.BlockSpec((slot_count, BLOCK, 2 * HEAD), lambda i, s: (0, 0, 0))
    grid_spec = pltpu.PrefetchScalarGridSpec(
        num_scalar_prefetch=1,
        grid=(rows,),
        in_specs=[row_spec, row_spec, full_spec],
        out_specs=[row_spec, row_spec, full_spec],
        scratch_shapes=[pltpu.VMEM((slot_count, BLOCK, 2 * HEAD), jnp.float32)],
    )
    out_shape = [
        jax.ShapeDtypeStruct((rows, BLOCK, HEAD), jnp.bfloat16),
        jax.ShapeDtypeStruct((rows, BLOCK, HEAD), jnp.bfloat16),
        jax.ShapeDtypeStruct((slot_count, BLOCK, 2 * HEAD), jnp.bfloat16),
    ]
    return pl.pallas_call(
        functools.partial(_attn_kernel, scale=scale),
        grid_spec=grid_spec,
        out_shape=out_shape,
        compiler_params=pltpu.CompilerParams(
            dimension_semantics=("arbitrary",), vmem_limit_bytes=48 * 1024 * 1024
        ),
    )(slots, queries, upstream, kv)


def on_device(tokens, projection, pattern, upstream):
    seq_count = lax.axis_size("seq")
    zero_count = lax.axis_size("zero")
    zero_index = lax.axis_index("zero")
    tok_rows = tokens.shape[0]
    model_width = tokens.shape[1]
    heads_here = HEADS // seq_count
    head_cols = heads_here * HEAD
    per_shard = tok_rows // BLOCK
    local_blocks = seq_count * per_shard
    score_scale = HEAD ** (-0.5)
    seq_index = lax.axis_index("seq")
    core = seq_index % 2
    first = core == 0
    pair = [(i, i ^ 1) for i in range(seq_count)]
    width = projection.shape[1] // 2
    w_mine = lax.dynamic_slice_in_dim(projection, core * width, width, axis=1)
    w_mine = lax.all_gather(w_mine, "zero", axis=0, tiled=True)
    w_other = lax.ppermute(w_mine, "seq", pair)
    half_d = model_width // 2
    t_halves = tokens.reshape(tok_rows, 2, half_d).transpose(1, 0, 2)
    t_send = jnp.tile(t_halves, (seq_count // 2, 1, 1))
    t_mine = lax.all_to_all(t_send, "seq", split_axis=0, concat_axis=0, tiled=True)
    t_mine = t_mine.reshape(seq_count * tok_rows, half_d)
    t_other = lax.ppermute(t_mine, "seq", pair)
    group_tokens = jnp.concatenate(
        [jnp.where(first, t_mine, t_other), jnp.where(first, t_other, t_mine)], axis=1
    )
    head_w = projection.reshape(projection.shape[0], 3, seq_count, head_cols)
    head_w = lax.dynamic_index_in_dim(head_w, seq_index, axis=2, keepdims=False)
    head_w = lax.all_gather(head_w, "zero", axis=0, tiled=True)
    queries = jnp.einsum(
        "td,dc->tc", group_tokens, head_w[:, 0], preferred_element_type=jnp.float32
    ).astype(jnp.bfloat16)
    kv_local = jnp.einsum(
        "td,dc->tc",
        group_tokens,
        head_w[:, 1:].reshape(-1, 2 * head_cols),
        preferred_element_type=jnp.float32,
    ).astype(jnp.bfloat16)
    kv_all = lax.all_gather(kv_local, "zero", axis=0, tiled=True)
    incoming = lax.all_to_all(
        upstream.reshape(tok_rows, seq_count, head_cols),
        "seq",
        split_axis=1,
        concat_axis=0,
        tiled=True,
    )
    local_ids = jnp.arange(local_blocks, dtype=jnp.int32)
    row_ids = (local_ids // per_shard * zero_count + zero_index) * per_shard + local_ids % per_shard
    row_lists = pattern[row_ids]
    shard_ids = row_lists // per_shard
    key_slots = (
        shard_ids % zero_count * local_blocks
        + shard_ids // zero_count * per_shard
        + row_lists % per_shard
    )

    out_blocks, query_grads, group_sums = block_attention(
        key_slots.reshape(local_blocks, NBK),
        queries.reshape(local_blocks, BLOCK, head_cols),
        incoming.reshape(local_blocks, BLOCK, head_cols),
        kv_all.reshape(-1, BLOCK, 2 * head_cols),
        score_scale,
    )
    attended = lax.all_to_all(
        out_blocks.reshape(local_blocks * BLOCK, 1, head_cols),
        "seq",
        split_axis=0,
        concat_axis=1,
        tiled=True,
    )
    attended = attended.reshape(tok_rows, seq_count * head_cols)
    group_sums = group_sums.reshape(zero_count, local_blocks * BLOCK, 2 * head_cols)
    group_sums = lax.all_to_all(group_sums, "zero", split_axis=0, concat_axis=0, tiled=True)
    kv_sum = jnp.sum(group_sums.astype(jnp.float32), axis=0).astype(jnp.bfloat16)
    local_grads = jnp.concatenate([query_grads.reshape(-1, head_cols), kv_sum], axis=1)
    local_grads = local_grads.reshape(local_blocks * BLOCK, 3, 1, head_cols)
    token_grads = lax.all_to_all(local_grads, "seq", split_axis=0, concat_axis=2, tiled=True)
    flat_grads = token_grads.reshape(tok_rows, 3 * seq_count * head_cols)
    g_mine = lax.dynamic_slice_in_dim(flat_grads, core * width, width, axis=1)
    g_other = lax.dynamic_slice_in_dim(flat_grads, (1 - core) * width, width, axis=1)
    token_gradient = (
        jnp.einsum("tc,dc->td", g_mine, w_mine, preferred_element_type=jnp.float32)
        + jnp.einsum("tc,dc->td", g_other, w_other, preferred_element_type=jnp.float32)
    ).astype(jnp.bfloat16)
    head_grads = local_grads.reshape(local_blocks * BLOCK, 3 * head_cols)
    head_part = jnp.einsum(
        "td,tc->dc", group_tokens, head_grads, preferred_element_type=jnp.float32
    )
    head_part = head_part.reshape(zero_count, -1, 3 * head_cols)
    head_part = lax.all_to_all(head_part, "zero", split_axis=0, concat_axis=0, tiled=True)
    own_rows = jnp.sum(head_part, axis=0)
    own_rows = own_rows.reshape(1, -1, 3, head_cols)
    gathered = lax.all_gather(own_rows, "seq", axis=0, tiled=True)
    weight_gradient = gathered.transpose(1, 2, 0, 3).reshape(-1, 3 * seq_count * head_cols)
    return (attended, token_gradient, weight_gradient)


def solution(mesh):
    return jax.shard_map(
        on_device,
        mesh=mesh,
        in_specs=(P(("seq", "zero"), None), P("zero", None), P(), P(("seq", "zero"), None)),
        out_specs=(P(("seq", "zero"), None), P(("seq", "zero"), None), P("zero", None)),
        check_vma=False,
    )
```

```python
import functools
import jax
import jax.numpy as jnp
from jax import lax
from jax.sharding import PartitionSpec as P
from jax.experimental import pallas as pl
from jax.experimental.pallas import tpu as pltpu

HEADS = 16
HEAD = 64
BLOCK = 128
NBK = 8


def _attn_kernel(slots_ref, q_ref, up_ref, kv_ref, out_ref, qg_ref, kvg_ref, acc_ref, *, scale):
    i = pl.program_id(0)

    @pl.when(i == 0)
    def _():
        acc_ref[...] = jnp.zeros(acc_ref.shape, acc_ref.dtype)

    q = q_ref[0]
    up = up_ref[0]
    ids = [slots_ref[i, j] for j in range(NBK)]
    blocks = [kv_ref[ids[j]] for j in range(NBK)]
    keys = jnp.concatenate([b[:, :HEAD] for b in blocks], axis=0)
    vals = jnp.concatenate([b[:, HEAD:] for b in blocks], axis=0)
    nt = (((1,), (1,)), ((), ()))
    tn = (((0,), (0,)), ((), ()))
    scores = lax.dot_general(q, keys, nt, preferred_element_type=jnp.float32) * scale
    row_max = jnp.max(scores, axis=-1, keepdims=True)
    exponent = jnp.exp(scores - row_max)
    prob_full = exponent / jnp.sum(exponent, axis=-1, keepdims=True)
    prob_low = prob_full.astype(jnp.bfloat16)
    out_ref[0] = jnp.dot(prob_low, vals, preferred_element_type=jnp.float32).astype(out_ref.dtype)
    prob_grad = lax.dot_general(up, vals, nt, preferred_element_type=jnp.float32)
    row_delta = jnp.sum(prob_full * prob_grad, axis=-1, keepdims=True)
    score_grad = (prob_full * (prob_grad - row_delta) * scale).astype(jnp.bfloat16)
    qg_ref[0] = jnp.dot(score_grad, keys, preferred_element_type=jnp.float32).astype(qg_ref.dtype)
    key_terms = lax.dot_general(score_grad, q, tn, preferred_element_type=jnp.float32)
    value_terms = lax.dot_general(prob_low, up, tn, preferred_element_type=jnp.float32)
    terms = jnp.concatenate([key_terms, value_terms], axis=1)
    for j in range(NBK):
        acc_ref[ids[j]] += terms[j * BLOCK:(j + 1) * BLOCK]

    @pl.when(i == pl.num_programs(0) - 1)
    def _():
        kvg_ref[...] = acc_ref[...].astype(kvg_ref.dtype)


def block_attention(slots, queries, upstream, kv, scale):
    rows = queries.shape[0]
    slot_count = kv.shape[0]
    row_spec = pl.BlockSpec((1, BLOCK, HEAD), lambda i, s: (i, 0, 0))
    full_spec = pl.BlockSpec((slot_count, BLOCK, 2 * HEAD), lambda i, s: (0, 0, 0))
    grid_spec = pltpu.PrefetchScalarGridSpec(
        num_scalar_prefetch=1,
        grid=(rows,),
        in_specs=[row_spec, row_spec, full_spec],
        out_specs=[row_spec, row_spec, full_spec],
        scratch_shapes=[pltpu.VMEM((slot_count, BLOCK, 2 * HEAD), jnp.float32)],
    )
    out_shape = [
        jax.ShapeDtypeStruct((rows, BLOCK, HEAD), jnp.bfloat16),
        jax.ShapeDtypeStruct((rows, BLOCK, HEAD), jnp.bfloat16),
        jax.ShapeDtypeStruct((slot_count, BLOCK, 2 * HEAD), jnp.bfloat16),
    ]
    return pl.pallas_call(
        functools.partial(_attn_kernel, scale=scale),
        grid_spec=grid_spec,
        out_shape=out_shape,
        compiler_params=pltpu.CompilerParams(
            dimension_semantics=("arbitrary",), vmem_limit_bytes=48 * 1024 * 1024
        ),
    )(slots, queries, upstream, kv)


def on_device(tokens, projection, pattern, upstream):
    seq_count = lax.axis_size("seq")
    zero_count = lax.axis_size("zero")
    zero_index = lax.axis_index("zero")
    tok_rows = tokens.shape[0]
    model_width = tokens.shape[1]
    heads_here = HEADS // seq_count
    head_cols = heads_here * HEAD
    per_shard = tok_rows // BLOCK
    local_blocks = seq_count * per_shard
    score_scale = HEAD ** (-0.5)
    seq_index = lax.axis_index("seq")
    core = seq_index % 2
    pair = [(i, i ^ 1) for i in range(seq_count)]
    width = projection.shape[1] // 2
    w_mine = lax.dynamic_slice_in_dim(projection, core * width, width, axis=1)
    w_mine = lax.all_gather(w_mine, "zero", axis=0, tiled=True)
    w_other = lax.ppermute(w_mine, "seq", pair)
    group_tokens = lax.all_gather(tokens, "seq", axis=0, tiled=True)
    head_w = projection.reshape(projection.shape[0], 3, seq_count, head_cols)
    head_w = lax.dynamic_index_in_dim(head_w, seq_index, axis=2, keepdims=False)
    head_w = lax.all_gather(head_w, "zero", axis=0, tiled=True)
    kv_local = jnp.einsum(
        "td,dc->tc",
        group_tokens,
        head_w[:, 1:].reshape(-1, 2 * head_cols),
        preferred_element_type=jnp.float32,
    ).astype(jnp.bfloat16)
    kv_local, group_tokens, upstream = lax.optimization_barrier((kv_local, group_tokens, upstream))
    queries = jnp.einsum(
        "td,dc->tc", group_tokens, head_w[:, 0], preferred_element_type=jnp.float32
    ).astype(jnp.bfloat16)
    kv_all = lax.all_gather(kv_local, "zero", axis=0, tiled=True)
    incoming = lax.all_to_all(
        upstream.reshape(tok_rows, seq_count, head_cols),
        "seq",
        split_axis=1,
        concat_axis=0,
        tiled=True,
    )
    local_ids = jnp.arange(local_blocks, dtype=jnp.int32)
    row_ids = (local_ids // per_shard * zero_count + zero_index) * per_shard + local_ids % per_shard
    row_lists = pattern[row_ids]
    shard_ids = row_lists // per_shard
    key_slots = (
        shard_ids % zero_count * local_blocks
        + shard_ids // zero_count * per_shard
        + row_lists % per_shard
    )

    out_blocks, query_grads, group_sums = block_attention(
        key_slots.reshape(local_blocks, NBK),
        queries.reshape(local_blocks, BLOCK, head_cols),
        incoming.reshape(local_blocks, BLOCK, head_cols),
        kv_all.reshape(-1, BLOCK, 2 * head_cols),
        score_scale,
    )
    attended = lax.all_to_all(
        out_blocks.reshape(local_blocks * BLOCK, 1, head_cols),
        "seq",
        split_axis=0,
        concat_axis=1,
        tiled=True,
    )
    attended = attended.reshape(tok_rows, seq_count * head_cols)
    group_sums = group_sums.reshape(zero_count, local_blocks * BLOCK, 2 * head_cols)
    group_sums = lax.all_to_all(group_sums, "zero", split_axis=0, concat_axis=0, tiled=True)
    kv_sum = jnp.sum(group_sums.astype(jnp.float32), axis=0).astype(jnp.bfloat16)
    local_grads = jnp.concatenate([query_grads.reshape(-1, head_cols), kv_sum], axis=1)
    local_grads = local_grads.reshape(local_blocks * BLOCK, 3, 1, head_cols)
    token_grads = lax.all_to_all(local_grads, "seq", split_axis=0, concat_axis=2, tiled=True)
    flat_grads = token_grads.reshape(tok_rows, 3 * seq_count * head_cols)
    g_mine = lax.dynamic_slice_in_dim(flat_grads, core * width, width, axis=1)
    g_other = lax.dynamic_slice_in_dim(flat_grads, (1 - core) * width, width, axis=1)
    token_gradient = (
        jnp.einsum("tc,dc->td", g_mine, w_mine, preferred_element_type=jnp.float32)
        + jnp.einsum("tc,dc->td", g_other, w_other, preferred_element_type=jnp.float32)
    ).astype(jnp.bfloat16)
    head_grads = local_grads.reshape(local_blocks * BLOCK, 3 * head_cols)
    head_part = jnp.einsum(
        "td,tc->dc", group_tokens, head_grads, preferred_element_type=jnp.float32
    )
    head_part = head_part.reshape(zero_count, -1, 3 * head_cols)
    head_part = lax.all_to_all(head_part, "zero", split_axis=0, concat_axis=0, tiled=True)
    own_rows = jnp.sum(head_part, axis=0)
    own_rows = own_rows.reshape(1, -1, 3, head_cols)
    gathered = lax.all_gather(own_rows, "seq", axis=0, tiled=True)
    weight_gradient = gathered.transpose(1, 2, 0, 3).reshape(-1, 3 * seq_count * head_cols)
    return (attended, token_gradient, weight_gradient)


def solution(mesh):
    return jax.shard_map(
        on_device,
        mesh=mesh,
        in_specs=(P(("seq", "zero"), None), P("zero", None), P(), P(("seq", "zero"), None)),
        out_specs=(P(("seq", "zero"), None), P(("seq", "zero"), None), P("zero", None)),
        check_vma=False,
    )
```

```python
import functools
import jax
import jax.numpy as jnp
from jax import lax
from jax.sharding import PartitionSpec as P
from jax.experimental import pallas as pl
from jax.experimental.pallas import tpu as pltpu

HEADS = 16
HEAD = 64
BLOCK = 128
NBK = 8


def _attn_kernel(slots_ref, q_ref, up_ref, kv_ref, out_ref, qg_ref, kvg_ref, acc_ref, *, scale):
    i = pl.program_id(0)

    @pl.when(i == 0)
    def _():
        acc_ref[...] = jnp.zeros(acc_ref.shape, acc_ref.dtype)

    q = q_ref[0]
    up = up_ref[0]
    ids = [slots_ref[i, j] for j in range(NBK)]
    blocks = [kv_ref[ids[j]] for j in range(NBK)]
    keys = jnp.concatenate([b[:, :HEAD] for b in blocks], axis=0)
    vals = jnp.concatenate([b[:, HEAD:] for b in blocks], axis=0)
    nt = (((1,), (1,)), ((), ()))
    tn = (((0,), (0,)), ((), ()))
    scores = lax.dot_general(q, keys, nt, preferred_element_type=jnp.float32) * scale
    row_max = jnp.max(scores, axis=-1, keepdims=True)
    exponent = jnp.exp(scores - row_max)
    prob_full = exponent / jnp.sum(exponent, axis=-1, keepdims=True)
    prob_low = prob_full.astype(jnp.bfloat16)
    out_ref[0] = jnp.dot(prob_low, vals, preferred_element_type=jnp.float32).astype(out_ref.dtype)
    prob_grad = lax.dot_general(up, vals, nt, preferred_element_type=jnp.float32)
    row_delta = jnp.sum(prob_full * prob_grad, axis=-1, keepdims=True)
    score_grad = (prob_full * (prob_grad - row_delta) * scale).astype(jnp.bfloat16)
    qg_ref[0] = jnp.dot(score_grad, keys, preferred_element_type=jnp.float32).astype(qg_ref.dtype)
    key_terms = lax.dot_general(score_grad, q, tn, preferred_element_type=jnp.float32)
    value_terms = lax.dot_general(prob_low, up, tn, preferred_element_type=jnp.float32)
    terms = jnp.concatenate([key_terms, value_terms], axis=1)
    for j in range(NBK):
        acc_ref[ids[j]] += terms[j * BLOCK:(j + 1) * BLOCK]

    @pl.when(i == pl.num_programs(0) - 1)
    def _():
        kvg_ref[...] = acc_ref[...].astype(kvg_ref.dtype)


def block_attention(slots, queries, upstream, kv, scale):
    rows = queries.shape[0]
    slot_count = kv.shape[0]
    row_spec = pl.BlockSpec((1, BLOCK, HEAD), lambda i, s: (i, 0, 0))
    full_spec = pl.BlockSpec((slot_count, BLOCK, 2 * HEAD), lambda i, s: (0, 0, 0))
    grid_spec = pltpu.PrefetchScalarGridSpec(
        num_scalar_prefetch=1,
        grid=(rows,),
        in_specs=[row_spec, row_spec, full_spec],
        out_specs=[row_spec, row_spec, full_spec],
        scratch_shapes=[pltpu.VMEM((slot_count, BLOCK, 2 * HEAD), jnp.float32)],
    )
    out_shape = [
        jax.ShapeDtypeStruct((rows, BLOCK, HEAD), jnp.bfloat16),
        jax.ShapeDtypeStruct((rows, BLOCK, HEAD), jnp.bfloat16),
        jax.ShapeDtypeStruct((slot_count, BLOCK, 2 * HEAD), jnp.bfloat16),
    ]
    return pl.pallas_call(
        functools.partial(_attn_kernel, scale=scale),
        grid_spec=grid_spec,
        out_shape=out_shape,
        compiler_params=pltpu.CompilerParams(
            dimension_semantics=("arbitrary",), vmem_limit_bytes=48 * 1024 * 1024
        ),
    )(slots, queries, upstream, kv)


def on_device(tokens, projection, pattern, upstream):
    seq_count = lax.axis_size("seq")
    zero_count = lax.axis_size("zero")
    zero_index = lax.axis_index("zero")
    tok_rows = tokens.shape[0]
    model_width = tokens.shape[1]
    heads_here = HEADS // seq_count
    head_cols = heads_here * HEAD
    per_shard = tok_rows // BLOCK
    local_blocks = seq_count * per_shard
    score_scale = HEAD ** (-0.5)
    seq_index = lax.axis_index("seq")
    core = seq_index % 2
    pair = [(i, i ^ 1) for i in range(seq_count)]
    width = projection.shape[1] // 2
    w_mine = lax.dynamic_slice_in_dim(projection, core * width, width, axis=1)
    w_mine = lax.all_gather(w_mine, "zero", axis=0, tiled=True)
    w_other = lax.ppermute(w_mine, "seq", pair)
    group_tokens = lax.all_gather(tokens, "seq", axis=0, tiled=True)
    head_w = projection.reshape(projection.shape[0], 3, seq_count, head_cols)
    head_w = lax.dynamic_index_in_dim(head_w, seq_index, axis=2, keepdims=False)
    head_w = lax.all_gather(head_w, "zero", axis=0, tiled=True)
    kv_local = jnp.einsum(
        "td,dc->tc",
        group_tokens,
        head_w[:, 1:].reshape(-1, 2 * head_cols),
        preferred_element_type=jnp.float32,
    ).astype(jnp.bfloat16)
    kv_local, group_tokens, upstream = lax.optimization_barrier((kv_local, group_tokens, upstream))
    queries = jnp.einsum(
        "td,dc->tc", group_tokens, head_w[:, 0], preferred_element_type=jnp.float32
    ).astype(jnp.bfloat16)
    kv_local = kv_local.reshape(local_blocks, BLOCK, 2 * head_cols)
    kv_all = lax.all_gather(kv_local, "zero", axis=0, tiled=True)
    incoming = lax.all_to_all(
        upstream.reshape(tok_rows, seq_count, head_cols),
        "seq",
        split_axis=1,
        concat_axis=0,
        tiled=True,
    )
    local_ids = jnp.arange(local_blocks, dtype=jnp.int32)
    row_ids = (local_ids // per_shard * zero_count + zero_index) * per_shard + local_ids % per_shard
    row_lists = pattern[row_ids]
    shard_ids = row_lists // per_shard
    key_slots = (
        shard_ids % zero_count * local_blocks
        + shard_ids // zero_count * per_shard
        + row_lists % per_shard
    )

    out_blocks, query_grads, group_sums = block_attention(
        key_slots.reshape(local_blocks, NBK),
        queries.reshape(local_blocks, BLOCK, head_cols),
        incoming.reshape(local_blocks, BLOCK, head_cols),
        kv_all,
        score_scale,
    )
    attended = lax.all_to_all(
        out_blocks.reshape(local_blocks * BLOCK, 1, head_cols),
        "seq",
        split_axis=0,
        concat_axis=1,
        tiled=True,
    )
    attended = attended.reshape(tok_rows, seq_count * head_cols)
    group_sums = group_sums.reshape(zero_count, local_blocks * BLOCK, 2 * head_cols)
    group_sums = lax.all_to_all(group_sums, "zero", split_axis=0, concat_axis=0, tiled=True)
    kv_sum = jnp.sum(group_sums.astype(jnp.float32), axis=0).astype(jnp.bfloat16)
    local_grads = jnp.concatenate([query_grads.reshape(-1, head_cols), kv_sum], axis=1)
    local_grads = local_grads.reshape(local_blocks * BLOCK, 3, 1, head_cols)
    token_grads = lax.all_to_all(local_grads, "seq", split_axis=0, concat_axis=2, tiled=True)
    flat_grads = token_grads.reshape(tok_rows, 3 * seq_count * head_cols)
    g_mine = lax.dynamic_slice_in_dim(flat_grads, core * width, width, axis=1)
    g_other = lax.dynamic_slice_in_dim(flat_grads, (1 - core) * width, width, axis=1)
    token_gradient = (
        jnp.einsum("tc,dc->td", g_mine, w_mine, preferred_element_type=jnp.float32)
        + jnp.einsum("tc,dc->td", g_other, w_other, preferred_element_type=jnp.float32)
    ).astype(jnp.bfloat16)
    head_grads = local_grads.reshape(local_blocks * BLOCK, 3 * head_cols)
    head_part = jnp.einsum(
        "td,tc->dc", group_tokens, head_grads, preferred_element_type=jnp.float32
    )
    head_part = head_part.reshape(zero_count, -1, 3 * head_cols)
    head_part = lax.all_to_all(head_part, "zero", split_axis=0, concat_axis=0, tiled=True)
    own_rows = jnp.sum(head_part, axis=0)
    own_rows = own_rows.reshape(1, -1, 3, head_cols)
    gathered = lax.all_gather(own_rows, "seq", axis=0, tiled=True)
    weight_gradient = gathered.transpose(1, 2, 0, 3).reshape(-1, 3 * seq_count * head_cols)
    return (attended, token_gradient, weight_gradient)


def solution(mesh):
    return jax.shard_map(
        on_device,
        mesh=mesh,
        in_specs=(P(("seq", "zero"), None), P("zero", None), P(), P(("seq", "zero"), None)),
        out_specs=(P(("seq", "zero"), None), P(("seq", "zero"), None), P("zero", None)),
        check_vma=False,
    )
```

```python
import functools
import jax
import jax.numpy as jnp
from jax import lax
from jax.sharding import PartitionSpec as P
from jax.experimental import pallas as pl
from jax.experimental.pallas import tpu as pltpu

HEADS = 16
HEAD = 64
BLOCK = 128
NBK = 8


def _attn_kernel(slots_ref, a_ids_ref, b_ids_ref, q_ref, up_ref, ka_ref, kb_ref, out_ref, qg_ref, kvg_ref, acc_ref, *, scale):
    i = pl.program_id(0)

    @pl.when(i == 0)
    def _():
        acc_ref[...] = jnp.zeros(acc_ref.shape, acc_ref.dtype)

    q = q_ref[0]
    up = up_ref[0]
    ids = [slots_ref[i, j] for j in range(NBK)]
    blocks = [
        jnp.where(a_ids_ref[i, j] >= 0, ka_ref[jnp.maximum(a_ids_ref[i, j], 0)], kb_ref[b_ids_ref[i, j]])
        for j in range(NBK)
    ]
    keys = jnp.concatenate([b[:, :HEAD] for b in blocks], axis=0)
    vals = jnp.concatenate([b[:, HEAD:] for b in blocks], axis=0)
    nt = (((1,), (1,)), ((), ()))
    tn = (((0,), (0,)), ((), ()))
    scores = lax.dot_general(q, keys, nt, preferred_element_type=jnp.float32) * scale
    row_max = jnp.max(scores, axis=-1, keepdims=True)
    exponent = jnp.exp(scores - row_max)
    prob_full = exponent / jnp.sum(exponent, axis=-1, keepdims=True)
    prob_low = prob_full.astype(jnp.bfloat16)
    out_ref[0] = jnp.dot(prob_low, vals, preferred_element_type=jnp.float32).astype(out_ref.dtype)
    prob_grad = lax.dot_general(up, vals, nt, preferred_element_type=jnp.float32)
    row_delta = jnp.sum(prob_full * prob_grad, axis=-1, keepdims=True)
    score_grad = (prob_full * (prob_grad - row_delta) * scale).astype(jnp.bfloat16)
    qg_ref[0] = jnp.dot(score_grad, keys, preferred_element_type=jnp.float32).astype(qg_ref.dtype)
    key_terms = lax.dot_general(score_grad, q, tn, preferred_element_type=jnp.float32)
    value_terms = lax.dot_general(prob_low, up, tn, preferred_element_type=jnp.float32)
    terms = jnp.concatenate([key_terms, value_terms], axis=1)
    for j in range(NBK):
        acc_ref[ids[j]] += terms[j * BLOCK:(j + 1) * BLOCK]

    @pl.when(i == pl.num_programs(0) - 1)
    def _():
        kvg_ref[...] = acc_ref[...].astype(kvg_ref.dtype)


def block_attention(slots, a_ids, b_ids, queries, upstream, kv_a, kv_b, scale):
    rows = queries.shape[0]
    slot_count = 2 * kv_a.shape[0]
    row_spec = pl.BlockSpec((1, BLOCK, HEAD), lambda i, s, a, b: (i, 0, 0))
    half_spec = pl.BlockSpec((slot_count // 2, BLOCK, 2 * HEAD), lambda i, s, a, b: (0, 0, 0))
    full_spec = pl.BlockSpec((slot_count, BLOCK, 2 * HEAD), lambda i, s, a, b: (0, 0, 0))
    grid_spec = pltpu.PrefetchScalarGridSpec(
        num_scalar_prefetch=3,
        grid=(rows,),
        in_specs=[row_spec, row_spec, half_spec, half_spec],
        out_specs=[row_spec, row_spec, full_spec],
        scratch_shapes=[pltpu.VMEM((slot_count, BLOCK, 2 * HEAD), jnp.float32)],
    )
    out_shape = [
        jax.ShapeDtypeStruct((rows, BLOCK, HEAD), jnp.bfloat16),
        jax.ShapeDtypeStruct((rows, BLOCK, HEAD), jnp.bfloat16),
        jax.ShapeDtypeStruct((slot_count, BLOCK, 2 * HEAD), jnp.bfloat16),
    ]
    return pl.pallas_call(
        functools.partial(_attn_kernel, scale=scale),
        grid_spec=grid_spec,
        out_shape=out_shape,
        compiler_params=pltpu.CompilerParams(
            dimension_semantics=("arbitrary",), vmem_limit_bytes=48 * 1024 * 1024
        ),
    )(slots, a_ids, b_ids, queries, upstream, kv_a, kv_b)


def on_device(tokens, projection, pattern, upstream):
    seq_count = lax.axis_size("seq")
    zero_count = lax.axis_size("zero")
    zero_index = lax.axis_index("zero")
    tok_rows = tokens.shape[0]
    model_width = tokens.shape[1]
    heads_here = HEADS // seq_count
    head_cols = heads_here * HEAD
    per_shard = tok_rows // BLOCK
    local_blocks = seq_count * per_shard
    score_scale = HEAD ** (-0.5)
    seq_index = lax.axis_index("seq")
    core = seq_index % 2
    pair = [(i, i ^ 1) for i in range(seq_count)]
    width = projection.shape[1] // 2
    w_mine = lax.dynamic_slice_in_dim(projection, core * width, width, axis=1)
    w_mine = lax.all_gather(w_mine, "zero", axis=0, tiled=True)
    w_other = lax.ppermute(w_mine, "seq", pair)
    group_tokens = lax.all_gather(tokens, "seq", axis=0, tiled=True)
    head_w = projection.reshape(projection.shape[0], 3, seq_count, head_cols)
    head_w = lax.dynamic_index_in_dim(head_w, seq_index, axis=2, keepdims=False)
    head_w = lax.all_gather(head_w, "zero", axis=0, tiled=True)
    kv_local = jnp.einsum(
        "td,dc->tc",
        group_tokens,
        head_w[:, 1:].reshape(-1, 2 * head_cols),
        preferred_element_type=jnp.float32,
    ).astype(jnp.bfloat16)
    kv_local, group_tokens, upstream = lax.optimization_barrier((kv_local, group_tokens, upstream))
    queries = jnp.einsum(
        "td,dc->tc", group_tokens, head_w[:, 0], preferred_element_type=jnp.float32
    ).astype(jnp.bfloat16)
    kv_local = kv_local.reshape(local_blocks, BLOCK, 2 * head_cols)
    split = local_blocks // 2
    kv_a = lax.all_gather(kv_local[:split], "zero", axis=0, tiled=True)
    kv_b = jnp.broadcast_to(kv_local[split:], (zero_count,) + kv_local[split:].shape)
    kv_b = lax.all_to_all(kv_b, "zero", split_axis=0, concat_axis=0, tiled=True)
    kv_b = kv_b.reshape(-1, BLOCK, 2 * head_cols)
    incoming = lax.all_to_all(
        upstream.reshape(tok_rows, seq_count, head_cols),
        "seq",
        split_axis=1,
        concat_axis=0,
        tiled=True,
    )
    local_ids = jnp.arange(local_blocks, dtype=jnp.int32)
    row_ids = (local_ids // per_shard * zero_count + zero_index) * per_shard + local_ids % per_shard
    row_lists = pattern[row_ids]
    shard_ids = row_lists // per_shard
    key_slots = (
        shard_ids % zero_count * local_blocks
        + shard_ids // zero_count * per_shard
        + row_lists % per_shard
    )

    key_slots = key_slots.reshape(local_blocks, NBK)
    slot_zero = key_slots // local_blocks
    slot_local = key_slots % local_blocks
    a_ids = jnp.where(slot_local < split, slot_zero * split + slot_local, -1)
    b_ids = slot_zero * (local_blocks - split) + jnp.maximum(slot_local - split, 0)
    out_blocks, query_grads, group_sums = block_attention(
        key_slots,
        a_ids,
        b_ids,
        queries.reshape(local_blocks, BLOCK, head_cols),
        incoming.reshape(local_blocks, BLOCK, head_cols),
        kv_a,
        kv_b,
        score_scale,
    )
    attended = lax.all_to_all(
        out_blocks.reshape(local_blocks * BLOCK, 1, head_cols),
        "seq",
        split_axis=0,
        concat_axis=1,
        tiled=True,
    )
    attended = attended.reshape(tok_rows, seq_count * head_cols)
    group_sums = group_sums.reshape(zero_count, local_blocks * BLOCK, 2 * head_cols)
    group_sums = lax.all_to_all(group_sums, "zero", split_axis=0, concat_axis=0, tiled=True)
    kv_sum = jnp.sum(group_sums.astype(jnp.float32), axis=0).astype(jnp.bfloat16)
    local_grads = jnp.concatenate([query_grads.reshape(-1, head_cols), kv_sum], axis=1)
    local_grads = local_grads.reshape(local_blocks * BLOCK, 3, 1, head_cols)
    token_grads = lax.all_to_all(local_grads, "seq", split_axis=0, concat_axis=2, tiled=True)
    flat_grads = token_grads.reshape(tok_rows, 3 * seq_count * head_cols)
    g_mine = lax.dynamic_slice_in_dim(flat_grads, core * width, width, axis=1)
    g_other = lax.dynamic_slice_in_dim(flat_grads, (1 - core) * width, width, axis=1)
    token_gradient = (
        jnp.einsum("tc,dc->td", g_mine, w_mine, preferred_element_type=jnp.float32)
        + jnp.einsum("tc,dc->td", g_other, w_other, preferred_element_type=jnp.float32)
    ).astype(jnp.bfloat16)
    head_grads = local_grads.reshape(local_blocks * BLOCK, 3 * head_cols)
    head_part = jnp.einsum(
        "td,tc->dc", group_tokens, head_grads, preferred_element_type=jnp.float32
    )
    head_part = head_part.reshape(zero_count, -1, 3 * head_cols)
    head_part = lax.all_to_all(head_part, "zero", split_axis=0, concat_axis=0, tiled=True)
    own_rows = jnp.sum(head_part, axis=0)
    own_rows = own_rows.reshape(1, -1, 3, head_cols)
    gathered = lax.all_gather(own_rows, "seq", axis=0, tiled=True)
    weight_gradient = gathered.transpose(1, 2, 0, 3).reshape(-1, 3 * seq_count * head_cols)
    return (attended, token_gradient, weight_gradient)


def solution(mesh):
    return jax.shard_map(
        on_device,
        mesh=mesh,
        in_specs=(P(("seq", "zero"), None), P("zero", None), P(), P(("seq", "zero"), None)),
        out_specs=(P(("seq", "zero"), None), P(("seq", "zero"), None), P("zero", None)),
        check_vma=False,
    )
```

```python
import functools
import jax
import jax.numpy as jnp
from jax import lax
from jax.sharding import PartitionSpec as P
from jax.experimental import pallas as pl
from jax.experimental.pallas import tpu as pltpu

HEADS = 16
HEAD = 64
BLOCK = 128
NBK = 8


def _attn_kernel(slots_ref, a_ids_ref, b_ids_ref, q_ref, up_ref, ka_ref, kb_ref, out_ref, qg_ref, kvg_ref, acc_ref, *, scale):
    i = pl.program_id(0)

    @pl.when(i == 0)
    def _():
        acc_ref[...] = jnp.zeros(acc_ref.shape, acc_ref.dtype)

    q = q_ref[0]
    up = up_ref[0]
    ids = [slots_ref[i, j] for j in range(NBK)]
    blocks = [
        jnp.where(a_ids_ref[i, j] >= 0, ka_ref[jnp.maximum(a_ids_ref[i, j], 0)], kb_ref[b_ids_ref[i, j]])
        for j in range(NBK)
    ]
    keys = jnp.concatenate([b[:, :HEAD] for b in blocks], axis=0)
    vals = jnp.concatenate([b[:, HEAD:] for b in blocks], axis=0)
    nt = (((1,), (1,)), ((), ()))
    tn = (((0,), (0,)), ((), ()))
    scores = lax.dot_general(q, keys, nt, preferred_element_type=jnp.float32) * scale
    row_max = jnp.max(scores, axis=-1, keepdims=True)
    exponent = jnp.exp(scores - row_max)
    prob_full = exponent / jnp.sum(exponent, axis=-1, keepdims=True)
    prob_low = prob_full.astype(jnp.bfloat16)
    out_ref[0] = jnp.dot(prob_low, vals, preferred_element_type=jnp.float32).astype(out_ref.dtype)
    prob_grad = lax.dot_general(up, vals, nt, preferred_element_type=jnp.float32)
    row_delta = jnp.sum(prob_full * prob_grad, axis=-1, keepdims=True)
    score_grad = (prob_full * (prob_grad - row_delta) * scale).astype(jnp.bfloat16)
    qg_ref[0] = jnp.dot(score_grad, keys, preferred_element_type=jnp.float32).astype(qg_ref.dtype)
    key_terms = lax.dot_general(score_grad, q, tn, preferred_element_type=jnp.float32)
    value_terms = lax.dot_general(prob_low, up, tn, preferred_element_type=jnp.float32)
    terms = jnp.concatenate([key_terms, value_terms], axis=1)
    for j in range(NBK):
        acc_ref[ids[j]] += terms[j * BLOCK:(j + 1) * BLOCK]

    @pl.when(i == pl.num_programs(0) - 1)
    def _():
        kvg_ref[...] = acc_ref[...].astype(kvg_ref.dtype)


def block_attention(slots, a_ids, b_ids, queries, upstream, kv_a, kv_b, scale):
    rows = queries.shape[0]
    slot_count = kv_a.shape[0] + kv_b.shape[0]
    row_spec = pl.BlockSpec((1, BLOCK, HEAD), lambda i, s, a, b: (i, 0, 0))
    a_spec = pl.BlockSpec((kv_a.shape[0], BLOCK, 2 * HEAD), lambda i, s, a, b: (0, 0, 0))
    b_spec = pl.BlockSpec((kv_b.shape[0], BLOCK, 2 * HEAD), lambda i, s, a, b: (0, 0, 0))
    full_spec = pl.BlockSpec((slot_count, BLOCK, 2 * HEAD), lambda i, s, a, b: (0, 0, 0))
    grid_spec = pltpu.PrefetchScalarGridSpec(
        num_scalar_prefetch=3,
        grid=(rows,),
        in_specs=[row_spec, row_spec, a_spec, b_spec],
        out_specs=[row_spec, row_spec, full_spec],
        scratch_shapes=[pltpu.VMEM((slot_count, BLOCK, 2 * HEAD), jnp.float32)],
    )
    out_shape = [
        jax.ShapeDtypeStruct((rows, BLOCK, HEAD), jnp.bfloat16),
        jax.ShapeDtypeStruct((rows, BLOCK, HEAD), jnp.bfloat16),
        jax.ShapeDtypeStruct((slot_count, BLOCK, 2 * HEAD), jnp.bfloat16),
    ]
    return pl.pallas_call(
        functools.partial(_attn_kernel, scale=scale),
        grid_spec=grid_spec,
        out_shape=out_shape,
        compiler_params=pltpu.CompilerParams(
            dimension_semantics=("arbitrary",), vmem_limit_bytes=48 * 1024 * 1024
        ),
    )(slots, a_ids, b_ids, queries, upstream, kv_a, kv_b)


def on_device(tokens, projection, pattern, upstream):
    seq_count = lax.axis_size("seq")
    zero_count = lax.axis_size("zero")
    zero_index = lax.axis_index("zero")
    tok_rows = tokens.shape[0]
    model_width = tokens.shape[1]
    heads_here = HEADS // seq_count
    head_cols = heads_here * HEAD
    per_shard = tok_rows // BLOCK
    local_blocks = seq_count * per_shard
    score_scale = HEAD ** (-0.5)
    seq_index = lax.axis_index("seq")
    core = seq_index % 2
    pair = [(i, i ^ 1) for i in range(seq_count)]
    width = projection.shape[1] // 2
    w_mine = lax.dynamic_slice_in_dim(projection, core * width, width, axis=1)
    w_mine = lax.all_gather(w_mine, "zero", axis=0, tiled=True)
    w_other = lax.ppermute(w_mine, "seq", pair)
    group_tokens = lax.all_gather(tokens, "seq", axis=0, tiled=True)
    head_w = projection.reshape(projection.shape[0], 3, seq_count, head_cols)
    head_w = lax.dynamic_index_in_dim(head_w, seq_index, axis=2, keepdims=False)
    head_w = lax.all_gather(head_w, "zero", axis=0, tiled=True)
    kv_local = jnp.einsum(
        "td,dc->tc",
        group_tokens,
        head_w[:, 1:].reshape(-1, 2 * head_cols),
        preferred_element_type=jnp.float32,
    ).astype(jnp.bfloat16)
    kv_local, group_tokens, upstream = lax.optimization_barrier((kv_local, group_tokens, upstream))
    queries = jnp.einsum(
        "td,dc->tc", group_tokens, head_w[:, 0], preferred_element_type=jnp.float32
    ).astype(jnp.bfloat16)
    kv_local = kv_local.reshape(local_blocks, BLOCK, 2 * head_cols)
    split = local_blocks // 4
    kv_a = lax.all_gather(kv_local[:split], "zero", axis=0, tiled=True)
    kv_b = jnp.broadcast_to(kv_local[split:], (zero_count,) + kv_local[split:].shape)
    kv_b = lax.all_to_all(kv_b, "zero", split_axis=0, concat_axis=0, tiled=True)
    kv_b = kv_b.reshape(-1, BLOCK, 2 * head_cols)
    incoming = lax.all_to_all(
        upstream.reshape(tok_rows, seq_count, head_cols),
        "seq",
        split_axis=1,
        concat_axis=0,
        tiled=True,
    )
    local_ids = jnp.arange(local_blocks, dtype=jnp.int32)
    row_ids = (local_ids // per_shard * zero_count + zero_index) * per_shard + local_ids % per_shard
    row_lists = pattern[row_ids]
    shard_ids = row_lists // per_shard
    key_slots = (
        shard_ids % zero_count * local_blocks
        + shard_ids // zero_count * per_shard
        + row_lists % per_shard
    )

    key_slots = key_slots.reshape(local_blocks, NBK)
    slot_zero = key_slots // local_blocks
    slot_local = key_slots % local_blocks
    a_ids = jnp.where(slot_local < split, slot_zero * split + slot_local, -1)
    b_ids = slot_zero * (local_blocks - split) + jnp.maximum(slot_local - split, 0)
    out_blocks, query_grads, group_sums = block_attention(
        key_slots,
        a_ids,
        b_ids,
        queries.reshape(local_blocks, BLOCK, head_cols),
        incoming.reshape(local_blocks, BLOCK, head_cols),
        kv_a,
        kv_b,
        score_scale,
    )
    attended = lax.all_to_all(
        out_blocks.reshape(local_blocks * BLOCK, 1, head_cols),
        "seq",
        split_axis=0,
        concat_axis=1,
        tiled=True,
    )
    attended = attended.reshape(tok_rows, seq_count * head_cols)
    group_sums = group_sums.reshape(zero_count, local_blocks * BLOCK, 2 * head_cols)
    group_sums = lax.all_to_all(group_sums, "zero", split_axis=0, concat_axis=0, tiled=True)
    kv_sum = jnp.sum(group_sums.astype(jnp.float32), axis=0).astype(jnp.bfloat16)
    local_grads = jnp.concatenate([query_grads.reshape(-1, head_cols), kv_sum], axis=1)
    local_grads = local_grads.reshape(local_blocks * BLOCK, 3, 1, head_cols)
    token_grads = lax.all_to_all(local_grads, "seq", split_axis=0, concat_axis=2, tiled=True)
    flat_grads = token_grads.reshape(tok_rows, 3 * seq_count * head_cols)
    g_mine = lax.dynamic_slice_in_dim(flat_grads, core * width, width, axis=1)
    g_other = lax.dynamic_slice_in_dim(flat_grads, (1 - core) * width, width, axis=1)
    token_gradient = (
        jnp.einsum("tc,dc->td", g_mine, w_mine, preferred_element_type=jnp.float32)
        + jnp.einsum("tc,dc->td", g_other, w_other, preferred_element_type=jnp.float32)
    ).astype(jnp.bfloat16)
    head_grads = local_grads.reshape(local_blocks * BLOCK, 3 * head_cols)
    head_part = jnp.einsum(
        "td,tc->dc", group_tokens, head_grads, preferred_element_type=jnp.float32
    )
    head_part = head_part.reshape(zero_count, -1, 3 * head_cols)
    head_part = lax.all_to_all(head_part, "zero", split_axis=0, concat_axis=0, tiled=True)
    own_rows = jnp.sum(head_part, axis=0)
    own_rows = own_rows.reshape(1, -1, 3, head_cols)
    gathered = lax.all_gather(own_rows, "seq", axis=0, tiled=True)
    weight_gradient = gathered.transpose(1, 2, 0, 3).reshape(-1, 3 * seq_count * head_cols)
    return (attended, token_gradient, weight_gradient)


def solution(mesh):
    return jax.shard_map(
        on_device,
        mesh=mesh,
        in_specs=(P(("seq", "zero"), None), P("zero", None), P(), P(("seq", "zero"), None)),
        out_specs=(P(("seq", "zero"), None), P(("seq", "zero"), None), P("zero", None)),
        check_vma=False,
    )
```

```python
import functools
import jax
import jax.numpy as jnp
from jax import lax
from jax.sharding import PartitionSpec as P
from jax.experimental import pallas as pl
from jax.experimental.pallas import tpu as pltpu

HEADS = 16
HEAD = 64
BLOCK = 128
NBK = 8


def _attn_kernel(slots_ref, a_ids_ref, b_ids_ref, q_ref, up_ref, ka_ref, kb_ref, out_ref, qg_ref, kvg_ref, acc_ref, *, scale):
    i = pl.program_id(0)

    @pl.when(i == 0)
    def _():
        acc_ref[...] = jnp.zeros(acc_ref.shape, acc_ref.dtype)

    q = q_ref[0]
    up = up_ref[0]
    ids = [slots_ref[i, j] for j in range(NBK)]
    blocks = [
        jnp.where(a_ids_ref[i, j] >= 0, ka_ref[jnp.maximum(a_ids_ref[i, j], 0)], kb_ref[b_ids_ref[i, j]])
        for j in range(NBK)
    ]
    keys = jnp.concatenate([b[:, :HEAD] for b in blocks], axis=0)
    vals = jnp.concatenate([b[:, HEAD:] for b in blocks], axis=0)
    nt = (((1,), (1,)), ((), ()))
    tn = (((0,), (0,)), ((), ()))
    scores = lax.dot_general(q, keys, nt, preferred_element_type=jnp.float32) * scale
    row_max = jnp.max(scores, axis=-1, keepdims=True)
    exponent = jnp.exp(scores - row_max)
    prob_full = exponent / jnp.sum(exponent, axis=-1, keepdims=True)
    prob_low = prob_full.astype(jnp.bfloat16)
    out_ref[0] = jnp.dot(prob_low, vals, preferred_element_type=jnp.float32).astype(out_ref.dtype)
    prob_grad = lax.dot_general(up, vals, nt, preferred_element_type=jnp.float32)
    row_delta = jnp.sum(prob_full * prob_grad, axis=-1, keepdims=True)
    score_grad = (prob_full * (prob_grad - row_delta) * scale).astype(jnp.bfloat16)
    qg_ref[0] = jnp.dot(score_grad, keys, preferred_element_type=jnp.float32).astype(qg_ref.dtype)
    key_terms = lax.dot_general(score_grad, q, tn, preferred_element_type=jnp.float32)
    value_terms = lax.dot_general(prob_low, up, tn, preferred_element_type=jnp.float32)
    terms = jnp.concatenate([key_terms, value_terms], axis=1)
    for j in range(NBK):
        acc_ref[ids[j]] += terms[j * BLOCK:(j + 1) * BLOCK]

    @pl.when(i == pl.num_programs(0) - 1)
    def _():
        kvg_ref[...] = acc_ref[...].astype(kvg_ref.dtype)


def block_attention(slots, a_ids, b_ids, queries, upstream, kv_a, kv_b, scale):
    rows = queries.shape[0]
    slot_count = 2 * kv_a.shape[0]
    row_spec = pl.BlockSpec((1, BLOCK, HEAD), lambda i, s, a, b: (i, 0, 0))
    half_spec = pl.BlockSpec((slot_count // 2, BLOCK, 2 * HEAD), lambda i, s, a, b: (0, 0, 0))
    full_spec = pl.BlockSpec((slot_count, BLOCK, 2 * HEAD), lambda i, s, a, b: (0, 0, 0))
    grid_spec = pltpu.PrefetchScalarGridSpec(
        num_scalar_prefetch=3,
        grid=(rows,),
        in_specs=[row_spec, row_spec, half_spec, half_spec],
        out_specs=[row_spec, row_spec, full_spec],
        scratch_shapes=[pltpu.VMEM((slot_count, BLOCK, 2 * HEAD), jnp.float32)],
    )
    out_shape = [
        jax.ShapeDtypeStruct((rows, BLOCK, HEAD), jnp.bfloat16),
        jax.ShapeDtypeStruct((rows, BLOCK, HEAD), jnp.bfloat16),
        jax.ShapeDtypeStruct((slot_count, BLOCK, 2 * HEAD), jnp.bfloat16),
    ]
    return pl.pallas_call(
        functools.partial(_attn_kernel, scale=scale),
        grid_spec=grid_spec,
        out_shape=out_shape,
        compiler_params=pltpu.CompilerParams(
            dimension_semantics=("arbitrary",), vmem_limit_bytes=48 * 1024 * 1024
        ),
    )(slots, a_ids, b_ids, queries, upstream, kv_a, kv_b)


def on_device(tokens, projection, pattern, upstream):
    seq_count = lax.axis_size("seq")
    zero_count = lax.axis_size("zero")
    zero_index = lax.axis_index("zero")
    tok_rows = tokens.shape[0]
    model_width = tokens.shape[1]
    heads_here = HEADS // seq_count
    head_cols = heads_here * HEAD
    per_shard = tok_rows // BLOCK
    local_blocks = seq_count * per_shard
    score_scale = HEAD ** (-0.5)
    seq_index = lax.axis_index("seq")
    core = seq_index % 2
    pair = [(i, i ^ 1) for i in range(seq_count)]
    width = projection.shape[1] // 2
    w_mine = lax.dynamic_slice_in_dim(projection, core * width, width, axis=1)
    w_mine = lax.all_gather(w_mine, "zero", axis=0, tiled=True)
    w_other = lax.ppermute(w_mine, "seq", pair)
    group_tokens = lax.all_gather(tokens, "seq", axis=0, tiled=True)
    head_w = projection.reshape(projection.shape[0], 3, seq_count, head_cols)
    head_w = lax.dynamic_index_in_dim(head_w, seq_index, axis=2, keepdims=False)
    head_w = lax.all_gather(head_w, "zero", axis=0, tiled=True)
    kv_local = jnp.einsum(
        "td,dc->tc",
        group_tokens,
        head_w[:, 1:].reshape(-1, 2 * head_cols),
        preferred_element_type=jnp.float32,
    ).astype(jnp.bfloat16)
    kv_local, group_tokens, upstream = lax.optimization_barrier((kv_local, group_tokens, upstream))
    queries = jnp.einsum(
        "td,dc->tc", group_tokens, head_w[:, 0], preferred_element_type=jnp.float32
    ).astype(jnp.bfloat16)
    kv_local = kv_local.reshape(local_blocks, BLOCK, 2 * head_cols)
    split = local_blocks // 2
    kv_a = lax.all_gather(kv_local[:split], "zero", axis=0, tiled=True)
    kv_b = jnp.broadcast_to(kv_local[split:], (zero_count,) + kv_local[split:].shape)
    kv_b = lax.all_to_all(kv_b, "zero", split_axis=0, concat_axis=0, tiled=True)
    kv_b = kv_b.reshape(-1, BLOCK, 2 * head_cols)
    incoming = lax.all_to_all(
        upstream.reshape(tok_rows, seq_count, head_cols),
        "seq",
        split_axis=1,
        concat_axis=0,
        tiled=True,
    )
    local_ids = jnp.arange(local_blocks, dtype=jnp.int32)
    row_ids = (local_ids // per_shard * zero_count + zero_index) * per_shard + local_ids % per_shard
    row_lists = pattern[row_ids]
    shard_ids = row_lists // per_shard
    key_slots = (
        shard_ids % zero_count * local_blocks
        + shard_ids // zero_count * per_shard
        + row_lists % per_shard
    )

    key_slots = key_slots.reshape(local_blocks, NBK)
    slot_zero = key_slots // local_blocks
    slot_local = key_slots % local_blocks
    a_ids = jnp.where(slot_local < split, slot_zero * split + slot_local, -1)
    b_ids = slot_zero * (local_blocks - split) + jnp.maximum(slot_local - split, 0)
    out_blocks, query_grads, group_sums = block_attention(
        key_slots,
        a_ids,
        b_ids,
        queries.reshape(local_blocks, BLOCK, head_cols),
        incoming.reshape(local_blocks, BLOCK, head_cols),
        kv_a,
        kv_b,
        score_scale,
    )
    group_sums = group_sums.reshape(zero_count, local_blocks * BLOCK, 2 * head_cols)
    group_sums = lax.all_to_all(group_sums, "zero", split_axis=0, concat_axis=0, tiled=True)
    kv_sum = jnp.sum(group_sums.astype(jnp.float32), axis=0).astype(jnp.bfloat16)
    local_grads = jnp.concatenate([query_grads.reshape(-1, head_cols), kv_sum], axis=1)
    outgoing = jnp.concatenate([out_blocks.reshape(-1, head_cols), local_grads], axis=1)
    outgoing = outgoing.reshape(local_blocks * BLOCK, 4, 1, head_cols)
    token_grads = lax.all_to_all(outgoing, "seq", split_axis=0, concat_axis=2, tiled=True)
    attended = token_grads[:, 0].reshape(tok_rows, seq_count * head_cols)
    flat_grads = token_grads[:, 1:].reshape(tok_rows, 3 * seq_count * head_cols)
    g_mine = lax.dynamic_slice_in_dim(flat_grads, core * width, width, axis=1)
    g_other = lax.dynamic_slice_in_dim(flat_grads, (1 - core) * width, width, axis=1)
    token_gradient = (
        jnp.einsum("tc,dc->td", g_mine, w_mine, preferred_element_type=jnp.float32)
        + jnp.einsum("tc,dc->td", g_other, w_other, preferred_element_type=jnp.float32)
    ).astype(jnp.bfloat16)
    head_grads = local_grads
    head_part = jnp.einsum(
        "td,tc->dc", group_tokens, head_grads, preferred_element_type=jnp.float32
    )
    head_part = head_part.reshape(zero_count, -1, 3 * head_cols)
    head_part = lax.all_to_all(head_part, "zero", split_axis=0, concat_axis=0, tiled=True)
    own_rows = jnp.sum(head_part, axis=0)
    own_rows = own_rows.reshape(1, -1, 3, head_cols)
    gathered = lax.all_gather(own_rows, "seq", axis=0, tiled=True)
    weight_gradient = gathered.transpose(1, 2, 0, 3).reshape(-1, 3 * seq_count * head_cols)
    return (attended, token_gradient, weight_gradient)


def solution(mesh):
    return jax.shard_map(
        on_device,
        mesh=mesh,
        in_specs=(P(("seq", "zero"), None), P("zero", None), P(), P(("seq", "zero"), None)),
        out_specs=(P(("seq", "zero"), None), P(("seq", "zero"), None), P("zero", None)),
        check_vma=False,
    )
```

```python
import functools
import jax
import jax.numpy as jnp
from jax import lax
from jax.sharding import PartitionSpec as P
from jax.experimental import pallas as pl
from jax.experimental.pallas import tpu as pltpu

HEADS = 16
HEAD = 64
BLOCK = 128
NBK = 8


def _attn_kernel(slots_ref, a_ids_ref, b_ids_ref, q_ref, up_ref, ka_ref, kb_ref, out_ref, qg_ref, kvg_ref, acc_ref, *, scale):
    i = pl.program_id(0)

    @pl.when(i == 0)
    def _():
        acc_ref[...] = jnp.zeros(acc_ref.shape, acc_ref.dtype)

    q = q_ref[0]
    up = up_ref[0]
    ids = [slots_ref[i, j] for j in range(NBK)]
    blocks = [
        jnp.where(a_ids_ref[i, j] >= 0, ka_ref[jnp.maximum(a_ids_ref[i, j], 0)], kb_ref[b_ids_ref[i, j]])
        for j in range(NBK)
    ]
    keys = jnp.concatenate([b[:, :HEAD] for b in blocks], axis=0)
    vals = jnp.concatenate([b[:, HEAD:] for b in blocks], axis=0)
    nt = (((1,), (1,)), ((), ()))
    tn = (((0,), (0,)), ((), ()))
    scores = lax.dot_general(q, keys, nt, preferred_element_type=jnp.float32) * scale
    row_max = jnp.max(scores, axis=-1, keepdims=True)
    exponent = jnp.exp(scores - row_max)
    prob_full = exponent / jnp.sum(exponent, axis=-1, keepdims=True)
    prob_low = prob_full.astype(jnp.bfloat16)
    out_ref[0] = jnp.dot(prob_low, vals, preferred_element_type=jnp.float32).astype(out_ref.dtype)
    prob_grad = lax.dot_general(up, vals, nt, preferred_element_type=jnp.float32)
    row_delta = jnp.sum(prob_full * prob_grad, axis=-1, keepdims=True)
    score_grad = (prob_full * (prob_grad - row_delta) * scale).astype(jnp.bfloat16)
    qg_ref[0] = jnp.dot(score_grad, keys, preferred_element_type=jnp.float32).astype(qg_ref.dtype)
    key_terms = lax.dot_general(score_grad, q, tn, preferred_element_type=jnp.float32)
    value_terms = lax.dot_general(prob_low, up, tn, preferred_element_type=jnp.float32)
    terms = jnp.concatenate([key_terms, value_terms], axis=1)
    for j in range(NBK):
        acc_ref[ids[j]] += terms[j * BLOCK:(j + 1) * BLOCK]

    @pl.when(i == pl.num_programs(0) - 1)
    def _():
        kvg_ref[...] = acc_ref[...].astype(kvg_ref.dtype)


def block_attention(slots, a_ids, b_ids, queries, upstream, kv_a, kv_b, scale):
    rows = queries.shape[0]
    slot_count = 2 * kv_a.shape[0]
    row_spec = pl.BlockSpec((1, BLOCK, HEAD), lambda i, s, a, b: (i, 0, 0))
    half_spec = pl.BlockSpec((slot_count // 2, BLOCK, 2 * HEAD), lambda i, s, a, b: (0, 0, 0))
    full_spec = pl.BlockSpec((slot_count, BLOCK, 2 * HEAD), lambda i, s, a, b: (0, 0, 0))
    grid_spec = pltpu.PrefetchScalarGridSpec(
        num_scalar_prefetch=3,
        grid=(rows,),
        in_specs=[row_spec, row_spec, half_spec, half_spec],
        out_specs=[row_spec, row_spec, full_spec],
        scratch_shapes=[pltpu.VMEM((slot_count, BLOCK, 2 * HEAD), jnp.float32)],
    )
    out_shape = [
        jax.ShapeDtypeStruct((rows, BLOCK, HEAD), jnp.bfloat16),
        jax.ShapeDtypeStruct((rows, BLOCK, HEAD), jnp.bfloat16),
        jax.ShapeDtypeStruct((slot_count, BLOCK, 2 * HEAD), jnp.bfloat16),
    ]
    return pl.pallas_call(
        functools.partial(_attn_kernel, scale=scale),
        grid_spec=grid_spec,
        out_shape=out_shape,
        compiler_params=pltpu.CompilerParams(
            dimension_semantics=("arbitrary",), vmem_limit_bytes=48 * 1024 * 1024
        ),
    )(slots, a_ids, b_ids, queries, upstream, kv_a, kv_b)


def on_device(tokens, projection, pattern, upstream):
    seq_count = lax.axis_size("seq")
    zero_count = lax.axis_size("zero")
    zero_index = lax.axis_index("zero")
    tok_rows = tokens.shape[0]
    model_width = tokens.shape[1]
    heads_here = HEADS // seq_count
    head_cols = heads_here * HEAD
    per_shard = tok_rows // BLOCK
    local_blocks = seq_count * per_shard
    score_scale = HEAD ** (-0.5)
    seq_index = lax.axis_index("seq")
    core = seq_index % 2
    pair = [(i, i ^ 1) for i in range(seq_count)]
    width = projection.shape[1] // 2
    w_mine = lax.dynamic_slice_in_dim(projection, core * width, width, axis=1)
    w_mine = lax.all_gather(w_mine, "zero", axis=0, tiled=True)
    w_other = lax.ppermute(w_mine, "seq", pair)
    half_rows = tok_rows // 2
    t_a = lax.all_gather(tokens[:half_rows], "seq", axis=0, tiled=True)
    t_b = jnp.broadcast_to(tokens[half_rows:], (seq_count, half_rows, model_width))
    t_b = lax.all_to_all(t_b, "seq", split_axis=0, concat_axis=0, tiled=True)
    group_tokens = jnp.concatenate(
        [t_a.reshape(seq_count, half_rows, model_width), t_b], axis=1
    ).reshape(seq_count * tok_rows, model_width)
    head_w = projection.reshape(projection.shape[0], 3, seq_count, head_cols)
    head_w = lax.dynamic_index_in_dim(head_w, seq_index, axis=2, keepdims=False)
    head_w = jnp.broadcast_to(head_w, (zero_count,) + head_w.shape)
    head_w = lax.all_to_all(head_w, "zero", split_axis=0, concat_axis=0, tiled=True)
    head_w = head_w.reshape(-1, 3, head_cols)
    kv_local = jnp.einsum(
        "td,dc->tc",
        group_tokens,
        head_w[:, 1:].reshape(-1, 2 * head_cols),
        preferred_element_type=jnp.float32,
    ).astype(jnp.bfloat16)
    kv_local, group_tokens, upstream = lax.optimization_barrier((kv_local, group_tokens, upstream))
    queries = jnp.einsum(
        "td,dc->tc", group_tokens, head_w[:, 0], preferred_element_type=jnp.float32
    ).astype(jnp.bfloat16)
    kv_local = kv_local.reshape(local_blocks, BLOCK, 2 * head_cols)
    split = local_blocks // 2
    kv_a = lax.all_gather(kv_local[:split], "zero", axis=0, tiled=True)
    kv_b = jnp.broadcast_to(kv_local[split:], (zero_count,) + kv_local[split:].shape)
    kv_b = lax.all_to_all(kv_b, "zero", split_axis=0, concat_axis=0, tiled=True)
    kv_b = kv_b.reshape(-1, BLOCK, 2 * head_cols)
    incoming = lax.all_to_all(
        upstream.reshape(tok_rows, seq_count, head_cols),
        "seq",
        split_axis=1,
        concat_axis=0,
        tiled=True,
    )
    local_ids = jnp.arange(local_blocks, dtype=jnp.int32)
    row_ids = (local_ids // per_shard * zero_count + zero_index) * per_shard + local_ids % per_shard
    row_lists = pattern[row_ids]
    shard_ids = row_lists // per_shard
    key_slots = (
        shard_ids % zero_count * local_blocks
        + shard_ids // zero_count * per_shard
        + row_lists % per_shard
    )

    key_slots = key_slots.reshape(local_blocks, NBK)
    slot_zero = key_slots // local_blocks
    slot_local = key_slots % local_blocks
    a_ids = jnp.where(slot_local < split, slot_zero * split + slot_local, -1)
    b_ids = slot_zero * (local_blocks - split) + jnp.maximum(slot_local - split, 0)
    out_blocks, query_grads, group_sums = block_attention(
        key_slots,
        a_ids,
        b_ids,
        queries.reshape(local_blocks, BLOCK, head_cols),
        incoming.reshape(local_blocks, BLOCK, head_cols),
        kv_a,
        kv_b,
        score_scale,
    )
    group_sums = group_sums.reshape(zero_count, local_blocks * BLOCK, 2 * head_cols)
    group_sums = lax.all_to_all(group_sums, "zero", split_axis=0, concat_axis=0, tiled=True)
    kv_sum = jnp.sum(group_sums.astype(jnp.float32), axis=0).astype(jnp.bfloat16)
    local_grads = jnp.concatenate([query_grads.reshape(-1, head_cols), kv_sum], axis=1)
    outgoing = jnp.concatenate([out_blocks.reshape(-1, head_cols), local_grads], axis=1)
    outgoing = outgoing.reshape(local_blocks * BLOCK, 4, 1, head_cols)
    token_grads = lax.all_to_all(outgoing, "seq", split_axis=0, concat_axis=2, tiled=True)
    attended = token_grads[:, 0].reshape(tok_rows, seq_count * head_cols)
    flat_grads = token_grads[:, 1:].reshape(tok_rows, 3 * seq_count * head_cols)
    g_mine = lax.dynamic_slice_in_dim(flat_grads, core * width, width, axis=1)
    g_other = lax.dynamic_slice_in_dim(flat_grads, (1 - core) * width, width, axis=1)
    token_gradient = (
        jnp.einsum("tc,dc->td", g_mine, w_mine, preferred_element_type=jnp.float32)
        + jnp.einsum("tc,dc->td", g_other, w_other, preferred_element_type=jnp.float32)
    ).astype(jnp.bfloat16)
    head_grads = local_grads
    head_part = jnp.einsum(
        "td,tc->dc", group_tokens, head_grads, preferred_element_type=jnp.float32
    )
    head_part = head_part.reshape(zero_count, -1, 3 * head_cols)
    head_part = lax.all_to_all(head_part, "zero", split_axis=0, concat_axis=0, tiled=True)
    own_rows = jnp.sum(head_part, axis=0)
    own_rows = own_rows.reshape(1, -1, 3, head_cols)
    gathered = lax.all_gather(own_rows, "seq", axis=0, tiled=True)
    weight_gradient = gathered.transpose(1, 2, 0, 3).reshape(-1, 3 * seq_count * head_cols)
    return (attended, token_gradient, weight_gradient)


def solution(mesh):
    return jax.shard_map(
        on_device,
        mesh=mesh,
        in_specs=(P(("seq", "zero"), None), P("zero", None), P(), P(("seq", "zero"), None)),
        out_specs=(P(("seq", "zero"), None), P(("seq", "zero"), None), P("zero", None)),
        check_vma=False,
    )
```

```python
import functools
import jax
import jax.numpy as jnp
from jax import lax
from jax.sharding import PartitionSpec as P
from jax.experimental import pallas as pl
from jax.experimental.pallas import tpu as pltpu

HEADS = 16
HEAD = 64
BLOCK = 128
NBK = 8


def _attn_kernel(slots_ref, a_ids_ref, b_ids_ref, q_ref, up_ref, ka_ref, kb_ref, out_ref, qg_ref, kvg_ref, acc_ref, *, scale):
    i = pl.program_id(0)

    @pl.when(i == 0)
    def _():
        acc_ref[...] = jnp.zeros(acc_ref.shape, acc_ref.dtype)

    q = q_ref[0]
    up = up_ref[0]
    ids = [slots_ref[i, j] for j in range(NBK)]
    blocks = [
        jnp.where(a_ids_ref[i, j] >= 0, ka_ref[jnp.maximum(a_ids_ref[i, j], 0)], kb_ref[b_ids_ref[i, j]])
        for j in range(NBK)
    ]
    keys = jnp.concatenate([b[:, :HEAD] for b in blocks], axis=0)
    vals = jnp.concatenate([b[:, HEAD:] for b in blocks], axis=0)
    nt = (((1,), (1,)), ((), ()))
    tn = (((0,), (0,)), ((), ()))
    scores = lax.dot_general(q, keys, nt, preferred_element_type=jnp.float32) * scale
    row_max = jnp.max(scores, axis=-1, keepdims=True)
    exponent = jnp.exp(scores - row_max)
    prob_full = exponent / jnp.sum(exponent, axis=-1, keepdims=True)
    prob_low = prob_full.astype(jnp.bfloat16)
    out_ref[0] = jnp.dot(prob_low, vals, preferred_element_type=jnp.float32).astype(out_ref.dtype)
    prob_grad = lax.dot_general(up, vals, nt, preferred_element_type=jnp.float32)
    row_delta = jnp.sum(prob_full * prob_grad, axis=-1, keepdims=True)
    score_grad = (prob_full * (prob_grad - row_delta) * scale).astype(jnp.bfloat16)
    qg_ref[0] = jnp.dot(score_grad, keys, preferred_element_type=jnp.float32).astype(qg_ref.dtype)
    key_terms = lax.dot_general(score_grad, q, tn, preferred_element_type=jnp.float32)
    value_terms = lax.dot_general(prob_low, up, tn, preferred_element_type=jnp.float32)
    terms = jnp.concatenate([key_terms, value_terms], axis=1)
    for j in range(NBK):
        acc_ref[ids[j]] += terms[j * BLOCK:(j + 1) * BLOCK]

    @pl.when(i == pl.num_programs(0) - 1)
    def _():
        kvg_ref[...] = acc_ref[...].astype(kvg_ref.dtype)


def block_attention(slots, a_ids, b_ids, queries, upstream, kv_a, kv_b, scale):
    rows = queries.shape[0]
    slot_count = 2 * kv_a.shape[0]
    row_spec = pl.BlockSpec((1, BLOCK, HEAD), lambda i, s, a, b: (i, 0, 0))
    half_spec = pl.BlockSpec((slot_count // 2, BLOCK, 2 * HEAD), lambda i, s, a, b: (0, 0, 0))
    full_spec = pl.BlockSpec((slot_count, BLOCK, 2 * HEAD), lambda i, s, a, b: (0, 0, 0))
    grid_spec = pltpu.PrefetchScalarGridSpec(
        num_scalar_prefetch=3,
        grid=(rows,),
        in_specs=[row_spec, row_spec, half_spec, half_spec],
        out_specs=[row_spec, row_spec, full_spec],
        scratch_shapes=[pltpu.VMEM((slot_count, BLOCK, 2 * HEAD), jnp.float32)],
    )
    out_shape = [
        jax.ShapeDtypeStruct((rows, BLOCK, HEAD), jnp.bfloat16),
        jax.ShapeDtypeStruct((rows, BLOCK, HEAD), jnp.bfloat16),
        jax.ShapeDtypeStruct((slot_count, BLOCK, 2 * HEAD), jnp.bfloat16),
    ]
    return pl.pallas_call(
        functools.partial(_attn_kernel, scale=scale),
        grid_spec=grid_spec,
        out_shape=out_shape,
        compiler_params=pltpu.CompilerParams(
            dimension_semantics=("arbitrary",), vmem_limit_bytes=48 * 1024 * 1024
        ),
    )(slots, a_ids, b_ids, queries, upstream, kv_a, kv_b)


def on_device(tokens, projection, pattern, upstream):
    seq_count = lax.axis_size("seq")
    zero_count = lax.axis_size("zero")
    zero_index = lax.axis_index("zero")
    tok_rows = tokens.shape[0]
    model_width = tokens.shape[1]
    heads_here = HEADS // seq_count
    head_cols = heads_here * HEAD
    per_shard = tok_rows // BLOCK
    local_blocks = seq_count * per_shard
    score_scale = HEAD ** (-0.5)
    seq_index = lax.axis_index("seq")
    core = seq_index % 2
    pair = [(i, i ^ 1) for i in range(seq_count)]
    width = projection.shape[1] // 2
    w_mine = lax.dynamic_slice_in_dim(projection, core * width, width, axis=1)
    w_mine = lax.all_gather(w_mine, "zero", axis=0, tiled=True)
    w_other = lax.ppermute(w_mine, "seq", pair)
    group_tokens = lax.all_gather(tokens, "seq", axis=0, tiled=True)
    head_w = projection.reshape(projection.shape[0], 3, seq_count, head_cols)
    head_w = lax.dynamic_index_in_dim(head_w, seq_index, axis=2, keepdims=False)
    head_w = lax.all_gather(head_w, "zero", axis=0, tiled=True)
    kv_local = jnp.einsum(
        "td,dc->tc",
        group_tokens,
        head_w[:, 1:].reshape(-1, 2 * head_cols),
        preferred_element_type=jnp.float32,
    ).astype(jnp.bfloat16)
    kv_local, group_tokens, upstream = lax.optimization_barrier((kv_local, group_tokens, upstream))
    queries = jnp.einsum(
        "td,dc->tc", group_tokens, head_w[:, 0], preferred_element_type=jnp.float32
    ).astype(jnp.bfloat16)
    kv_local = kv_local.reshape(local_blocks, BLOCK, 2 * head_cols)
    split = local_blocks // 2
    kv_a = lax.all_gather(kv_local[:split], "zero", axis=0, tiled=True)
    kv_b = jnp.broadcast_to(kv_local[split:], (zero_count,) + kv_local[split:].shape)
    kv_b = lax.all_to_all(kv_b, "zero", split_axis=0, concat_axis=0, tiled=True)
    kv_b = kv_b.reshape(-1, BLOCK, 2 * head_cols)
    incoming = lax.all_to_all(
        upstream.reshape(tok_rows, seq_count, head_cols),
        "seq",
        split_axis=1,
        concat_axis=0,
        tiled=True,
    )
    local_ids = jnp.arange(local_blocks, dtype=jnp.int32)
    row_ids = (local_ids // per_shard * zero_count + zero_index) * per_shard + local_ids % per_shard
    row_lists = pattern[row_ids]
    shard_ids = row_lists // per_shard
    key_slots = (
        shard_ids % zero_count * local_blocks
        + shard_ids // zero_count * per_shard
        + row_lists % per_shard
    )

    key_slots = key_slots.reshape(local_blocks, NBK)
    slot_zero = key_slots // local_blocks
    slot_local = key_slots % local_blocks
    a_ids = jnp.where(slot_local < split, slot_zero * split + slot_local, -1)
    b_ids = slot_zero * (local_blocks - split) + jnp.maximum(slot_local - split, 0)
    out_blocks, query_grads, group_sums = block_attention(
        key_slots,
        a_ids,
        b_ids,
        queries.reshape(local_blocks, BLOCK, head_cols),
        incoming.reshape(local_blocks, BLOCK, head_cols),
        kv_a,
        kv_b,
        score_scale,
    )
    group_sums = group_sums.reshape(zero_count, local_blocks, BLOCK, 2 * head_cols)
    part_a = lax.all_to_all(group_sums[:, :split], "zero", split_axis=0, concat_axis=0, tiled=True)
    sum_a = jnp.sum(part_a.astype(jnp.float32), axis=0)
    part_b = group_sums[:, split:]
    sum_b = lax.dynamic_index_in_dim(part_b, zero_index, axis=0, keepdims=False).astype(jnp.float32)
    for shift in range(1, zero_count):
        dest = (zero_index + shift) % zero_count
        piece = lax.dynamic_index_in_dim(part_b, dest, axis=0, keepdims=False)
        ring = [(i, (i + shift) % zero_count) for i in range(zero_count)]
        sum_b = sum_b + lax.ppermute(piece, "zero", ring).astype(jnp.float32)
    kv_sum = jnp.concatenate([sum_a, sum_b], axis=0).astype(jnp.bfloat16)
    kv_sum = kv_sum.reshape(local_blocks * BLOCK, 2 * head_cols)
    local_grads = jnp.concatenate([query_grads.reshape(-1, head_cols), kv_sum], axis=1)
    outgoing = jnp.concatenate([out_blocks.reshape(-1, head_cols), local_grads], axis=1)
    outgoing = outgoing.reshape(local_blocks * BLOCK, 4, 1, head_cols)
    token_grads = lax.all_to_all(outgoing, "seq", split_axis=0, concat_axis=2, tiled=True)
    attended = token_grads[:, 0].reshape(tok_rows, seq_count * head_cols)
    flat_grads = token_grads[:, 1:].reshape(tok_rows, 3 * seq_count * head_cols)
    g_mine = lax.dynamic_slice_in_dim(flat_grads, core * width, width, axis=1)
    g_other = lax.dynamic_slice_in_dim(flat_grads, (1 - core) * width, width, axis=1)
    token_gradient = (
        jnp.einsum("tc,dc->td", g_mine, w_mine, preferred_element_type=jnp.float32)
        + jnp.einsum("tc,dc->td", g_other, w_other, preferred_element_type=jnp.float32)
    ).astype(jnp.bfloat16)
    head_grads = local_grads
    head_part = jnp.einsum(
        "td,tc->dc", group_tokens, head_grads, preferred_element_type=jnp.float32
    )
    head_part = head_part.reshape(zero_count, -1, 3 * head_cols)
    head_part = lax.all_to_all(head_part, "zero", split_axis=0, concat_axis=0, tiled=True)
    own_rows = jnp.sum(head_part, axis=0)
    own_rows = own_rows.reshape(1, -1, 3, head_cols)
    gathered = lax.all_gather(own_rows, "seq", axis=0, tiled=True)
    weight_gradient = gathered.transpose(1, 2, 0, 3).reshape(-1, 3 * seq_count * head_cols)
    return (attended, token_gradient, weight_gradient)


def solution(mesh):
    return jax.shard_map(
        on_device,
        mesh=mesh,
        in_specs=(P(("seq", "zero"), None), P("zero", None), P(), P(("seq", "zero"), None)),
        out_specs=(P(("seq", "zero"), None), P(("seq", "zero"), None), P("zero", None)),
        check_vma=False,
    )
```

```python
import functools
import jax
import jax.numpy as jnp
from jax import lax
from jax.sharding import PartitionSpec as P
from jax.experimental import pallas as pl
from jax.experimental.pallas import tpu as pltpu

HEADS = 16
HEAD = 64
BLOCK = 128
NBK = 8


def _attn_kernel(slots_ref, a_ids_ref, b_ids_ref, q_ref, up_ref, ka_ref, kb_ref, out_ref, qg_ref, kvg_ref, acc_ref, *, scale):
    i = pl.program_id(0)

    @pl.when(i == 0)
    def _():
        acc_ref[...] = jnp.zeros(acc_ref.shape, acc_ref.dtype)

    q = q_ref[0]
    up = up_ref[0]
    ids = [slots_ref[i, j] for j in range(NBK)]
    blocks = [
        jnp.where(a_ids_ref[i, j] >= 0, ka_ref[jnp.maximum(a_ids_ref[i, j], 0)], kb_ref[b_ids_ref[i, j]])
        for j in range(NBK)
    ]
    keys = jnp.concatenate([b[:, :HEAD] for b in blocks], axis=0)
    vals = jnp.concatenate([b[:, HEAD:] for b in blocks], axis=0)
    nt = (((1,), (1,)), ((), ()))
    tn = (((0,), (0,)), ((), ()))
    scores = lax.dot_general(q, keys, nt, preferred_element_type=jnp.float32) * scale
    row_max = jnp.max(scores, axis=-1, keepdims=True)
    exponent = jnp.exp(scores - row_max)
    prob_full = exponent / jnp.sum(exponent, axis=-1, keepdims=True)
    prob_low = prob_full.astype(jnp.bfloat16)
    out_ref[0] = jnp.dot(prob_low, vals, preferred_element_type=jnp.float32).astype(out_ref.dtype)
    prob_grad = lax.dot_general(up, vals, nt, preferred_element_type=jnp.float32)
    row_delta = jnp.sum(prob_full * prob_grad, axis=-1, keepdims=True)
    score_grad = (prob_full * (prob_grad - row_delta) * scale).astype(jnp.bfloat16)
    qg_ref[0] = jnp.dot(score_grad, keys, preferred_element_type=jnp.float32).astype(qg_ref.dtype)
    key_terms = lax.dot_general(score_grad, q, tn, preferred_element_type=jnp.float32)
    value_terms = lax.dot_general(prob_low, up, tn, preferred_element_type=jnp.float32)
    terms = jnp.concatenate([key_terms, value_terms], axis=1)
    for j in range(NBK):
        acc_ref[ids[j]] += terms[j * BLOCK:(j + 1) * BLOCK]

    @pl.when(i == pl.num_programs(0) - 1)
    def _():
        kvg_ref[...] = acc_ref[...].astype(kvg_ref.dtype)


def block_attention(slots, a_ids, b_ids, queries, upstream, kv_a, kv_b, scale):
    rows = queries.shape[0]
    slot_count = 2 * kv_a.shape[0]
    row_spec = pl.BlockSpec((1, BLOCK, HEAD), lambda i, s, a, b: (i, 0, 0))
    half_spec = pl.BlockSpec((slot_count // 2, BLOCK, 2 * HEAD), lambda i, s, a, b: (0, 0, 0))
    full_spec = pl.BlockSpec((slot_count, BLOCK, 2 * HEAD), lambda i, s, a, b: (0, 0, 0))
    grid_spec = pltpu.PrefetchScalarGridSpec(
        num_scalar_prefetch=3,
        grid=(rows,),
        in_specs=[row_spec, row_spec, half_spec, half_spec],
        out_specs=[row_spec, row_spec, full_spec],
        scratch_shapes=[pltpu.VMEM((slot_count, BLOCK, 2 * HEAD), jnp.float32)],
    )
    out_shape = [
        jax.ShapeDtypeStruct((rows, BLOCK, HEAD), jnp.bfloat16),
        jax.ShapeDtypeStruct((rows, BLOCK, HEAD), jnp.bfloat16),
        jax.ShapeDtypeStruct((slot_count, BLOCK, 2 * HEAD), jnp.bfloat16),
    ]
    return pl.pallas_call(
        functools.partial(_attn_kernel, scale=scale),
        grid_spec=grid_spec,
        out_shape=out_shape,
        compiler_params=pltpu.CompilerParams(
            dimension_semantics=("arbitrary",), vmem_limit_bytes=48 * 1024 * 1024
        ),
    )(slots, a_ids, b_ids, queries, upstream, kv_a, kv_b)


def on_device(tokens, projection, pattern, upstream):
    seq_count = lax.axis_size("seq")
    zero_count = lax.axis_size("zero")
    zero_index = lax.axis_index("zero")
    tok_rows = tokens.shape[0]
    model_width = tokens.shape[1]
    heads_here = HEADS // seq_count
    head_cols = heads_here * HEAD
    per_shard = tok_rows // BLOCK
    local_blocks = seq_count * per_shard
    score_scale = HEAD ** (-0.5)
    seq_index = lax.axis_index("seq")
    core = seq_index % 2
    pair = [(i, i ^ 1) for i in range(seq_count)]
    width = projection.shape[1] // 2
    w_mine = lax.dynamic_slice_in_dim(projection, core * width, width, axis=1)
    w_mine = lax.all_gather(w_mine, "zero", axis=0, tiled=True)
    w_other = lax.ppermute(w_mine, "seq", pair)
    group_tokens = lax.all_gather(tokens, "seq", axis=0, tiled=True)
    head_w = projection.reshape(projection.shape[0], 3, seq_count, head_cols)
    head_w = lax.dynamic_index_in_dim(head_w, seq_index, axis=2, keepdims=False)
    head_w = lax.all_gather(head_w, "zero", axis=0, tiled=True)
    kv_local = jnp.einsum(
        "td,dc->tc",
        group_tokens,
        head_w[:, 1:].reshape(-1, 2 * head_cols),
        preferred_element_type=jnp.float32,
    ).astype(jnp.bfloat16)
    kv_local, group_tokens, upstream = lax.optimization_barrier((kv_local, group_tokens, upstream))
    queries = jnp.einsum(
        "td,dc->tc", group_tokens, head_w[:, 0], preferred_element_type=jnp.float32
    ).astype(jnp.bfloat16)
    kv_local = kv_local.reshape(local_blocks, BLOCK, 2 * head_cols)
    split = local_blocks // 2
    kv_a = lax.all_gather(kv_local[:split], "zero", axis=0, tiled=True)
    kv_b = jnp.broadcast_to(kv_local[split:], (zero_count,) + kv_local[split:].shape)
    kv_b = lax.all_to_all(kv_b, "zero", split_axis=0, concat_axis=0, tiled=True)
    kv_b = kv_b.reshape(-1, BLOCK, 2 * head_cols)
    incoming = lax.all_to_all(
        upstream.reshape(tok_rows, seq_count, head_cols),
        "seq",
        split_axis=1,
        concat_axis=0,
        tiled=True,
    )
    local_ids = jnp.arange(local_blocks, dtype=jnp.int32)
    row_ids = (local_ids // per_shard * zero_count + zero_index) * per_shard + local_ids % per_shard
    row_lists = pattern[row_ids]
    shard_ids = row_lists // per_shard
    key_slots = (
        shard_ids % zero_count * local_blocks
        + shard_ids // zero_count * per_shard
        + row_lists % per_shard
    )

    key_slots = key_slots.reshape(local_blocks, NBK)
    slot_zero = key_slots // local_blocks
    slot_local = key_slots % local_blocks
    a_ids = jnp.where(slot_local < split, slot_zero * split + slot_local, -1)
    b_ids = slot_zero * (local_blocks - split) + jnp.maximum(slot_local - split, 0)
    out_blocks, query_grads, group_sums = block_attention(
        key_slots,
        a_ids,
        b_ids,
        queries.reshape(local_blocks, BLOCK, head_cols),
        incoming.reshape(local_blocks, BLOCK, head_cols),
        kv_a,
        kv_b,
        score_scale,
    )
    group_sums = group_sums.reshape(zero_count, local_blocks * BLOCK, 2 * head_cols)
    group_sums = lax.all_to_all(group_sums, "zero", split_axis=0, concat_axis=0, tiled=True)
    kv_sum = jnp.sum(group_sums.astype(jnp.float32), axis=0).astype(jnp.bfloat16)
    local_grads = jnp.concatenate([query_grads.reshape(-1, head_cols), kv_sum], axis=1)
    outgoing = jnp.concatenate([out_blocks.reshape(-1, head_cols), local_grads], axis=1)
    outgoing = outgoing.reshape(local_blocks * BLOCK, 4, 1, head_cols)
    token_grads = lax.all_to_all(outgoing, "seq", split_axis=0, concat_axis=2, tiled=True)
    attended = token_grads[:, 0].reshape(tok_rows, seq_count * head_cols)
    flat_grads = token_grads[:, 1:].reshape(tok_rows, 3 * seq_count * head_cols)
    g_mine = lax.dynamic_slice_in_dim(flat_grads, core * width, width, axis=1)
    g_other = lax.dynamic_slice_in_dim(flat_grads, (1 - core) * width, width, axis=1)
    token_gradient = (
        jnp.einsum("tc,dc->td", g_mine, w_mine, preferred_element_type=jnp.float32)
        + jnp.einsum("tc,dc->td", g_other, w_other, preferred_element_type=jnp.float32)
    ).astype(jnp.bfloat16)
    head_grads = local_grads
    head_part = jnp.einsum(
        "td,tc->dc", group_tokens, head_grads, preferred_element_type=jnp.float32
    )
    head_part = head_part.reshape(zero_count, -1, 3 * head_cols)
    head_part = lax.all_to_all(head_part, "zero", split_axis=0, concat_axis=0, tiled=True)
    own_rows = jnp.sum(head_part, axis=0)
    own_rows = own_rows.reshape(-1, 3, head_cols)
    gathered = lax.all_gather(own_rows, "seq", axis=2, tiled=False)
    weight_gradient = gathered.reshape(-1, 3 * seq_count * head_cols)
    return (attended, token_gradient, weight_gradient)


def solution(mesh):
    return jax.shard_map(
        on_device,
        mesh=mesh,
        in_specs=(P(("seq", "zero"), None), P("zero", None), P(), P(("seq", "zero"), None)),
        out_specs=(P(("seq", "zero"), None), P(("seq", "zero"), None), P("zero", None)),
        check_vma=False,
    )
```

```python
import functools
import jax
import jax.numpy as jnp
from jax import lax
from jax.sharding import PartitionSpec as P
from jax.experimental import pallas as pl
from jax.experimental.pallas import tpu as pltpu

HEADS = 16
HEAD = 64
BLOCK = 128
NBK = 8


def _attn_kernel(slots_ref, a_ids_ref, b_ids_ref, q_ref, up_ref, ka_ref, kb_ref, out_ref, qg_ref, kvg_ref, acc_ref, *, scale):
    i = pl.program_id(0)

    @pl.when(i == 0)
    def _():
        acc_ref[...] = jnp.zeros(acc_ref.shape, acc_ref.dtype)

    q = q_ref[0]
    up = up_ref[0]
    ids = [slots_ref[i, j] for j in range(NBK)]
    blocks = [
        jnp.where(a_ids_ref[i, j] >= 0, ka_ref[jnp.maximum(a_ids_ref[i, j], 0)], kb_ref[b_ids_ref[i, j]])
        for j in range(NBK)
    ]
    keys = jnp.concatenate([b[:, :HEAD] for b in blocks], axis=0)
    vals = jnp.concatenate([b[:, HEAD:] for b in blocks], axis=0)
    nt = (((1,), (1,)), ((), ()))
    tn = (((0,), (0,)), ((), ()))
    scores = lax.dot_general(q * scale, keys, nt, preferred_element_type=jnp.float32)
    row_max = jnp.max(scores, axis=-1, keepdims=True)
    exponent = jnp.exp(scores - row_max)
    prob_full = exponent * (1.0 / jnp.sum(exponent, axis=-1, keepdims=True))
    prob_low = prob_full.astype(jnp.bfloat16)
    out_ref[0] = jnp.dot(prob_low, vals, preferred_element_type=jnp.float32).astype(out_ref.dtype)
    prob_grad = lax.dot_general(up, vals, nt, preferred_element_type=jnp.float32)
    row_delta = jnp.sum(prob_full * prob_grad, axis=-1, keepdims=True)
    score_grad = (prob_full * (prob_grad - row_delta) * scale).astype(jnp.bfloat16)
    qg_ref[0] = jnp.dot(score_grad, keys, preferred_element_type=jnp.float32).astype(qg_ref.dtype)
    key_terms = lax.dot_general(score_grad, q, tn, preferred_element_type=jnp.float32)
    value_terms = lax.dot_general(prob_low, up, tn, preferred_element_type=jnp.float32)
    terms = jnp.concatenate([key_terms, value_terms], axis=1)
    for j in range(NBK):
        acc_ref[ids[j]] += terms[j * BLOCK:(j + 1) * BLOCK]

    @pl.when(i == pl.num_programs(0) - 1)
    def _():
        kvg_ref[...] = acc_ref[...].astype(kvg_ref.dtype)


def block_attention(slots, a_ids, b_ids, queries, upstream, kv_a, kv_b, scale):
    rows = queries.shape[0]
    slot_count = 2 * kv_a.shape[0]
    row_spec = pl.BlockSpec((1, BLOCK, HEAD), lambda i, s, a, b: (i, 0, 0))
    half_spec = pl.BlockSpec((slot_count // 2, BLOCK, 2 * HEAD), lambda i, s, a, b: (0, 0, 0))
    full_spec = pl.BlockSpec((slot_count, BLOCK, 2 * HEAD), lambda i, s, a, b: (0, 0, 0))
    grid_spec = pltpu.PrefetchScalarGridSpec(
        num_scalar_prefetch=3,
        grid=(rows,),
        in_specs=[row_spec, row_spec, half_spec, half_spec],
        out_specs=[row_spec, row_spec, full_spec],
        scratch_shapes=[pltpu.VMEM((slot_count, BLOCK, 2 * HEAD), jnp.float32)],
    )
    out_shape = [
        jax.ShapeDtypeStruct((rows, BLOCK, HEAD), jnp.bfloat16),
        jax.ShapeDtypeStruct((rows, BLOCK, HEAD), jnp.bfloat16),
        jax.ShapeDtypeStruct((slot_count, BLOCK, 2 * HEAD), jnp.bfloat16),
    ]
    return pl.pallas_call(
        functools.partial(_attn_kernel, scale=scale),
        grid_spec=grid_spec,
        out_shape=out_shape,
        compiler_params=pltpu.CompilerParams(
            dimension_semantics=("arbitrary",), vmem_limit_bytes=48 * 1024 * 1024
        ),
    )(slots, a_ids, b_ids, queries, upstream, kv_a, kv_b)


def on_device(tokens, projection, pattern, upstream):
    seq_count = lax.axis_size("seq")
    zero_count = lax.axis_size("zero")
    zero_index = lax.axis_index("zero")
    tok_rows = tokens.shape[0]
    model_width = tokens.shape[1]
    heads_here = HEADS // seq_count
    head_cols = heads_here * HEAD
    per_shard = tok_rows // BLOCK
    local_blocks = seq_count * per_shard
    score_scale = HEAD ** (-0.5)
    seq_index = lax.axis_index("seq")
    core = seq_index % 2
    pair = [(i, i ^ 1) for i in range(seq_count)]
    width = projection.shape[1] // 2
    w_mine = lax.dynamic_slice_in_dim(projection, core * width, width, axis=1)
    w_mine = lax.all_gather(w_mine, "zero", axis=0, tiled=True)
    w_other = lax.ppermute(w_mine, "seq", pair)
    group_tokens = lax.all_gather(tokens, "seq", axis=0, tiled=True)
    head_w = projection.reshape(projection.shape[0], 3, seq_count, head_cols)
    head_w = lax.dynamic_index_in_dim(head_w, seq_index, axis=2, keepdims=False)
    head_w = lax.all_gather(head_w, "zero", axis=0, tiled=True)
    kv_local = jnp.einsum(
        "td,dc->tc",
        group_tokens,
        head_w[:, 1:].reshape(-1, 2 * head_cols),
        preferred_element_type=jnp.float32,
    ).astype(jnp.bfloat16)
    kv_local, group_tokens, upstream = lax.optimization_barrier((kv_local, group_tokens, upstream))
    queries = jnp.einsum(
        "td,dc->tc", group_tokens, head_w[:, 0], preferred_element_type=jnp.float32
    ).astype(jnp.bfloat16)
    kv_local = kv_local.reshape(local_blocks, BLOCK, 2 * head_cols)
    split = local_blocks // 2
    kv_a = lax.all_gather(kv_local[:split], "zero", axis=0, tiled=True)
    kv_b = jnp.broadcast_to(kv_local[split:], (zero_count,) + kv_local[split:].shape)
    kv_b = lax.all_to_all(kv_b, "zero", split_axis=0, concat_axis=0, tiled=True)
    kv_b = kv_b.reshape(-1, BLOCK, 2 * head_cols)
    incoming = lax.all_to_all(
        upstream.reshape(tok_rows, seq_count, head_cols),
        "seq",
        split_axis=1,
        concat_axis=0,
        tiled=True,
    )
    local_ids = jnp.arange(local_blocks, dtype=jnp.int32)
    row_ids = (local_ids // per_shard * zero_count + zero_index) * per_shard + local_ids % per_shard
    row_lists = pattern[row_ids]
    shard_ids = row_lists // per_shard
    key_slots = (
        shard_ids % zero_count * local_blocks
        + shard_ids // zero_count * per_shard
        + row_lists % per_shard
    )

    key_slots = key_slots.reshape(local_blocks, NBK)
    slot_zero = key_slots // local_blocks
    slot_local = key_slots % local_blocks
    a_ids = jnp.where(slot_local < split, slot_zero * split + slot_local, -1)
    b_ids = slot_zero * (local_blocks - split) + jnp.maximum(slot_local - split, 0)
    out_blocks, query_grads, group_sums = block_attention(
        key_slots,
        a_ids,
        b_ids,
        queries.reshape(local_blocks, BLOCK, head_cols),
        incoming.reshape(local_blocks, BLOCK, head_cols),
        kv_a,
        kv_b,
        score_scale,
    )
    group_sums = group_sums.reshape(zero_count, local_blocks * BLOCK, 2 * head_cols)
    group_sums = lax.all_to_all(group_sums, "zero", split_axis=0, concat_axis=0, tiled=True)
    kv_sum = jnp.sum(group_sums.astype(jnp.float32), axis=0).astype(jnp.bfloat16)
    local_grads = jnp.concatenate([query_grads.reshape(-1, head_cols), kv_sum], axis=1)
    outgoing = jnp.concatenate([out_blocks.reshape(-1, head_cols), local_grads], axis=1)
    outgoing = outgoing.reshape(local_blocks * BLOCK, 4, 1, head_cols)
    token_grads = lax.all_to_all(outgoing, "seq", split_axis=0, concat_axis=2, tiled=True)
    attended = token_grads[:, 0].reshape(tok_rows, seq_count * head_cols)
    flat_grads = token_grads[:, 1:].reshape(tok_rows, 3 * seq_count * head_cols)
    g_mine = lax.dynamic_slice_in_dim(flat_grads, core * width, width, axis=1)
    g_other = lax.dynamic_slice_in_dim(flat_grads, (1 - core) * width, width, axis=1)
    token_gradient = (
        jnp.einsum("tc,dc->td", g_mine, w_mine, preferred_element_type=jnp.float32)
        + jnp.einsum("tc,dc->td", g_other, w_other, preferred_element_type=jnp.float32)
    ).astype(jnp.bfloat16)
    head_grads = local_grads
    head_part = jnp.einsum(
        "td,tc->dc", group_tokens, head_grads, preferred_element_type=jnp.float32
    )
    head_part = head_part.reshape(zero_count, -1, 3 * head_cols)
    head_part = lax.all_to_all(head_part, "zero", split_axis=0, concat_axis=0, tiled=True)
    own_rows = jnp.sum(head_part, axis=0)
    own_rows = own_rows.reshape(1, -1, 3, head_cols)
    gathered = lax.all_gather(own_rows, "seq", axis=0, tiled=True)
    weight_gradient = gathered.transpose(1, 2, 0, 3).reshape(-1, 3 * seq_count * head_cols)
    return (attended, token_gradient, weight_gradient)


def solution(mesh):
    return jax.shard_map(
        on_device,
        mesh=mesh,
        in_specs=(P(("seq", "zero"), None), P("zero", None), P(), P(("seq", "zero"), None)),
        out_specs=(P(("seq", "zero"), None), P(("seq", "zero"), None), P("zero", None)),
        check_vma=False,
    )
```

```python
import functools
import jax
import jax.numpy as jnp
from jax import lax
from jax.sharding import PartitionSpec as P
from jax.experimental import pallas as pl
from jax.experimental.pallas import tpu as pltpu

HEADS = 16
HEAD = 64
BLOCK = 128
NBK = 8
ROWS_PER_STEP = 2


def _attn_kernel(slots_ref, a_ids_ref, b_ids_ref, q_ref, up_ref, ka_ref, kb_ref, out_ref, qg_ref, kvg_ref, acc_ref, *, scale):
    i = pl.program_id(0)

    @pl.when(i == 0)
    def _():
        acc_ref[...] = jnp.zeros(acc_ref.shape, acc_ref.dtype)

    for r in range(ROWS_PER_STEP):
        row = i * ROWS_PER_STEP + r
        q = q_ref[r]
        up = up_ref[r]
        ids = [slots_ref[row, j] for j in range(NBK)]
        blocks = [
            jnp.where(a_ids_ref[row, j] >= 0, ka_ref[jnp.maximum(a_ids_ref[row, j], 0)], kb_ref[b_ids_ref[row, j]])
            for j in range(NBK)
        ]
        keys = jnp.concatenate([b[:, :HEAD] for b in blocks], axis=0)
        vals = jnp.concatenate([b[:, HEAD:] for b in blocks], axis=0)
        nt = (((1,), (1,)), ((), ()))
        tn = (((0,), (0,)), ((), ()))
        scores = lax.dot_general(q, keys, nt, preferred_element_type=jnp.float32) * scale
        row_max = jnp.max(scores, axis=-1, keepdims=True)
        exponent = jnp.exp(scores - row_max)
        prob_full = exponent / jnp.sum(exponent, axis=-1, keepdims=True)
        prob_low = prob_full.astype(jnp.bfloat16)
        out_ref[r] = jnp.dot(prob_low, vals, preferred_element_type=jnp.float32).astype(out_ref.dtype)
        prob_grad = lax.dot_general(up, vals, nt, preferred_element_type=jnp.float32)
        row_delta = jnp.sum(prob_full * prob_grad, axis=-1, keepdims=True)
        score_grad = (prob_full * (prob_grad - row_delta) * scale).astype(jnp.bfloat16)
        qg_ref[r] = jnp.dot(score_grad, keys, preferred_element_type=jnp.float32).astype(qg_ref.dtype)
        key_terms = lax.dot_general(score_grad, q, tn, preferred_element_type=jnp.float32)
        value_terms = lax.dot_general(prob_low, up, tn, preferred_element_type=jnp.float32)
        terms = jnp.concatenate([key_terms, value_terms], axis=1)
        for j in range(NBK):
            acc_ref[ids[j]] += terms[j * BLOCK:(j + 1) * BLOCK]

    @pl.when(i == pl.num_programs(0) - 1)
    def _():
        kvg_ref[...] = acc_ref[...].astype(kvg_ref.dtype)


def block_attention(slots, a_ids, b_ids, queries, upstream, kv_a, kv_b, scale):
    rows = queries.shape[0]
    slot_count = 2 * kv_a.shape[0]
    row_spec = pl.BlockSpec((ROWS_PER_STEP, BLOCK, HEAD), lambda i, s, a, b: (i, 0, 0))
    half_spec = pl.BlockSpec((slot_count // 2, BLOCK, 2 * HEAD), lambda i, s, a, b: (0, 0, 0))
    full_spec = pl.BlockSpec((slot_count, BLOCK, 2 * HEAD), lambda i, s, a, b: (0, 0, 0))
    grid_spec = pltpu.PrefetchScalarGridSpec(
        num_scalar_prefetch=3,
        grid=(rows // ROWS_PER_STEP,),
        in_specs=[row_spec, row_spec, half_spec, half_spec],
        out_specs=[row_spec, row_spec, full_spec],
        scratch_shapes=[pltpu.VMEM((slot_count, BLOCK, 2 * HEAD), jnp.float32)],
    )
    out_shape = [
        jax.ShapeDtypeStruct((rows, BLOCK, HEAD), jnp.bfloat16),
        jax.ShapeDtypeStruct((rows, BLOCK, HEAD), jnp.bfloat16),
        jax.ShapeDtypeStruct((slot_count, BLOCK, 2 * HEAD), jnp.bfloat16),
    ]
    return pl.pallas_call(
        functools.partial(_attn_kernel, scale=scale),
        grid_spec=grid_spec,
        out_shape=out_shape,
        compiler_params=pltpu.CompilerParams(
            dimension_semantics=("arbitrary",), vmem_limit_bytes=48 * 1024 * 1024
        ),
    )(slots, a_ids, b_ids, queries, upstream, kv_a, kv_b)


def on_device(tokens, projection, pattern, upstream):
    seq_count = lax.axis_size("seq")
    zero_count = lax.axis_size("zero")
    zero_index = lax.axis_index("zero")
    tok_rows = tokens.shape[0]
    model_width = tokens.shape[1]
    heads_here = HEADS // seq_count
    head_cols = heads_here * HEAD
    per_shard = tok_rows // BLOCK
    local_blocks = seq_count * per_shard
    score_scale = HEAD ** (-0.5)
    seq_index = lax.axis_index("seq")
    core = seq_index % 2
    pair = [(i, i ^ 1) for i in range(seq_count)]
    width = projection.shape[1] // 2
    w_mine = lax.dynamic_slice_in_dim(projection, core * width, width, axis=1)
    w_mine = lax.all_gather(w_mine, "zero", axis=0, tiled=True)
    w_other = lax.ppermute(w_mine, "seq", pair)
    group_tokens = lax.all_gather(tokens, "seq", axis=0, tiled=True)
    head_w = projection.reshape(projection.shape[0], 3, seq_count, head_cols)
    head_w = lax.dynamic_index_in_dim(head_w, seq_index, axis=2, keepdims=False)
    head_w = lax.all_gather(head_w, "zero", axis=0, tiled=True)
    kv_local = jnp.einsum(
        "td,dc->tc",
        group_tokens,
        head_w[:, 1:].reshape(-1, 2 * head_cols),
        preferred_element_type=jnp.float32,
    ).astype(jnp.bfloat16)
    kv_local, group_tokens, upstream = lax.optimization_barrier((kv_local, group_tokens, upstream))
    queries = jnp.einsum(
        "td,dc->tc", group_tokens, head_w[:, 0], preferred_element_type=jnp.float32
    ).astype(jnp.bfloat16)
    kv_local = kv_local.reshape(local_blocks, BLOCK, 2 * head_cols)
    split = local_blocks // 2
    kv_a = lax.all_gather(kv_local[:split], "zero", axis=0, tiled=True)
    kv_b = jnp.broadcast_to(kv_local[split:], (zero_count,) + kv_local[split:].shape)
    kv_b = lax.all_to_all(kv_b, "zero", split_axis=0, concat_axis=0, tiled=True)
    kv_b = kv_b.reshape(-1, BLOCK, 2 * head_cols)
    incoming = lax.all_to_all(
        upstream.reshape(tok_rows, seq_count, head_cols),
        "seq",
        split_axis=1,
        concat_axis=0,
        tiled=True,
    )
    local_ids = jnp.arange(local_blocks, dtype=jnp.int32)
    row_ids = (local_ids // per_shard * zero_count + zero_index) * per_shard + local_ids % per_shard
    row_lists = pattern[row_ids]
    shard_ids = row_lists // per_shard
    key_slots = (
        shard_ids % zero_count * local_blocks
        + shard_ids // zero_count * per_shard
        + row_lists % per_shard
    )

    key_slots = key_slots.reshape(local_blocks, NBK)
    slot_zero = key_slots // local_blocks
    slot_local = key_slots % local_blocks
    a_ids = jnp.where(slot_local < split, slot_zero * split + slot_local, -1)
    b_ids = slot_zero * (local_blocks - split) + jnp.maximum(slot_local - split, 0)
    out_blocks, query_grads, group_sums = block_attention(
        key_slots,
        a_ids,
        b_ids,
        queries.reshape(local_blocks, BLOCK, head_cols),
        incoming.reshape(local_blocks, BLOCK, head_cols),
        kv_a,
        kv_b,
        score_scale,
    )
    group_sums = group_sums.reshape(zero_count, local_blocks * BLOCK, 2 * head_cols)
    group_sums = lax.all_to_all(group_sums, "zero", split_axis=0, concat_axis=0, tiled=True)
    kv_sum = jnp.sum(group_sums.astype(jnp.float32), axis=0).astype(jnp.bfloat16)
    local_grads = jnp.concatenate([query_grads.reshape(-1, head_cols), kv_sum], axis=1)
    outgoing = jnp.concatenate([out_blocks.reshape(-1, head_cols), local_grads], axis=1)
    outgoing = outgoing.reshape(local_blocks * BLOCK, 4, 1, head_cols)
    token_grads = lax.all_to_all(outgoing, "seq", split_axis=0, concat_axis=2, tiled=True)
    attended = token_grads[:, 0].reshape(tok_rows, seq_count * head_cols)
    flat_grads = token_grads[:, 1:].reshape(tok_rows, 3 * seq_count * head_cols)
    g_mine = lax.dynamic_slice_in_dim(flat_grads, core * width, width, axis=1)
    g_other = lax.dynamic_slice_in_dim(flat_grads, (1 - core) * width, width, axis=1)
    token_gradient = (
        jnp.einsum("tc,dc->td", g_mine, w_mine, preferred_element_type=jnp.float32)
        + jnp.einsum("tc,dc->td", g_other, w_other, preferred_element_type=jnp.float32)
    ).astype(jnp.bfloat16)
    head_grads = local_grads
    head_part = jnp.einsum(
        "td,tc->dc", group_tokens, head_grads, preferred_element_type=jnp.float32
    )
    head_part = head_part.reshape(zero_count, -1, 3 * head_cols)
    head_part = lax.all_to_all(head_part, "zero", split_axis=0, concat_axis=0, tiled=True)
    own_rows = jnp.sum(head_part, axis=0)
    own_rows = own_rows.reshape(1, -1, 3, head_cols)
    gathered = lax.all_gather(own_rows, "seq", axis=0, tiled=True)
    weight_gradient = gathered.transpose(1, 2, 0, 3).reshape(-1, 3 * seq_count * head_cols)
    return (attended, token_gradient, weight_gradient)


def solution(mesh):
    return jax.shard_map(
        on_device,
        mesh=mesh,
        in_specs=(P(("seq", "zero"), None), P("zero", None), P(), P(("seq", "zero"), None)),
        out_specs=(P(("seq", "zero"), None), P(("seq", "zero"), None), P("zero", None)),
        check_vma=False,
    )
```

```python
import functools
import jax
import jax.numpy as jnp
from jax import lax
from jax.sharding import PartitionSpec as P
from jax.experimental import pallas as pl
from jax.experimental.pallas import tpu as pltpu

HEADS = 16
HEAD = 64
BLOCK = 128
NBK = 8
ROWS_PER_STEP = 2


def _attn_kernel(slots_ref, a_ids_ref, b_ids_ref, q_ref, up_ref, ka_ref, kb_ref, out_ref, qg_ref, kvg_ref, acc_ref, *, scale):
    i = pl.program_id(0)

    @pl.when(i == 0)
    def _():
        acc_ref[...] = jnp.zeros(acc_ref.shape, acc_ref.dtype)

    for r in range(ROWS_PER_STEP):
        row = i * ROWS_PER_STEP + r
        q = q_ref[r]
        up = up_ref[r]
        ids = [slots_ref[row, j] for j in range(NBK)]
        blocks = [
            jnp.where(a_ids_ref[row, j] >= 0, ka_ref[jnp.maximum(a_ids_ref[row, j], 0)], kb_ref[b_ids_ref[row, j]])
            for j in range(NBK)
        ]
        keys = jnp.concatenate([b[:, :HEAD] for b in blocks], axis=0)
        vals = jnp.concatenate([b[:, HEAD:] for b in blocks], axis=0)
        nt = (((1,), (1,)), ((), ()))
        tn = (((0,), (0,)), ((), ()))
        scores = lax.dot_general(q, keys, nt, preferred_element_type=jnp.float32) * scale
        row_max = jnp.max(scores, axis=-1, keepdims=True)
        exponent = jnp.exp(scores - row_max)
        prob_full = exponent / jnp.sum(exponent, axis=-1, keepdims=True)
        prob_low = prob_full.astype(jnp.bfloat16)
        out_ref[r] = jnp.dot(prob_low, vals, preferred_element_type=jnp.float32).astype(out_ref.dtype)
        prob_grad = lax.dot_general(up, vals, nt, preferred_element_type=jnp.float32)
        row_delta = jnp.sum(prob_full * prob_grad, axis=-1, keepdims=True)
        score_grad = (prob_full * (prob_grad - row_delta) * scale).astype(jnp.bfloat16)
        qg_ref[r] = jnp.dot(score_grad, keys, preferred_element_type=jnp.float32).astype(qg_ref.dtype)
        key_terms = lax.dot_general(score_grad, q, tn, preferred_element_type=jnp.float32)
        value_terms = lax.dot_general(prob_low, up, tn, preferred_element_type=jnp.float32)
        terms = jnp.concatenate([key_terms, value_terms], axis=1)
        for j in range(NBK):
            acc_ref[ids[j]] += terms[j * BLOCK:(j + 1) * BLOCK]

    @pl.when(i == pl.num_programs(0) - 1)
    def _():
        kvg_ref[...] = acc_ref[...].astype(kvg_ref.dtype)


def block_attention(slots, a_ids, b_ids, queries, upstream, kv_a, kv_b, scale):
    rows = queries.shape[0]
    slot_count = kv_b.shape[0]
    row_spec = pl.BlockSpec((ROWS_PER_STEP, BLOCK, HEAD), lambda i, s, a, b: (i, 0, 0))
    half_spec = pl.BlockSpec((kv_a.shape[0], BLOCK, 2 * HEAD), lambda i, s, a, b: (0, 0, 0))
    full_spec = pl.BlockSpec((slot_count, BLOCK, 2 * HEAD), lambda i, s, a, b: (0, 0, 0))
    grid_spec = pltpu.PrefetchScalarGridSpec(
        num_scalar_prefetch=3,
        grid=(rows // ROWS_PER_STEP,),
        in_specs=[row_spec, row_spec, half_spec, half_spec],
        out_specs=[row_spec, row_spec, full_spec],
        scratch_shapes=[pltpu.VMEM((slot_count, BLOCK, 2 * HEAD), jnp.float32)],
    )
    out_shape = [
        jax.ShapeDtypeStruct((rows, BLOCK, HEAD), jnp.bfloat16),
        jax.ShapeDtypeStruct((rows, BLOCK, HEAD), jnp.bfloat16),
        jax.ShapeDtypeStruct((slot_count, BLOCK, 2 * HEAD), jnp.bfloat16),
    ]
    return pl.pallas_call(
        functools.partial(_attn_kernel, scale=scale),
        grid_spec=grid_spec,
        out_shape=out_shape,
        compiler_params=pltpu.CompilerParams(
            dimension_semantics=("arbitrary",), vmem_limit_bytes=48 * 1024 * 1024
        ),
    )(slots, a_ids, b_ids, queries, upstream, kv_a, kv_b)


def on_device(tokens, projection, pattern, upstream):
    seq_count = lax.axis_size("seq")
    zero_count = lax.axis_size("zero")
    zero_index = lax.axis_index("zero")
    tok_rows = tokens.shape[0]
    model_width = tokens.shape[1]
    heads_here = HEADS // seq_count
    head_cols = heads_here * HEAD
    per_shard = tok_rows // BLOCK
    local_blocks = seq_count * per_shard
    score_scale = HEAD ** (-0.5)
    seq_index = lax.axis_index("seq")
    core = seq_index % 2
    pair = [(i, i ^ 1) for i in range(seq_count)]
    width = projection.shape[1] // 2
    w_mine = lax.dynamic_slice_in_dim(projection, core * width, width, axis=1)
    w_mine = lax.all_gather(w_mine, "zero", axis=0, tiled=True)
    w_other = lax.ppermute(w_mine, "seq", pair)
    group_tokens = lax.all_gather(tokens, "seq", axis=0, tiled=True)
    head_w = projection.reshape(projection.shape[0], 3, seq_count, head_cols)
    head_w = lax.dynamic_index_in_dim(head_w, seq_index, axis=2, keepdims=False)
    head_w = lax.all_gather(head_w, "zero", axis=0, tiled=True)
    kv_local = jnp.einsum(
        "td,dc->tc",
        group_tokens,
        head_w[:, 1:].reshape(-1, 2 * head_cols),
        preferred_element_type=jnp.float32,
    ).astype(jnp.bfloat16)
    kv_local, group_tokens, upstream = lax.optimization_barrier((kv_local, group_tokens, upstream))
    queries = jnp.einsum(
        "td,dc->tc", group_tokens, head_w[:, 0], preferred_element_type=jnp.float32
    ).astype(jnp.bfloat16)
    kv_local = kv_local.reshape(local_blocks, BLOCK, 2 * head_cols)
    split = 0
    kv_b = jnp.broadcast_to(kv_local[split:], (zero_count,) + kv_local[split:].shape)
    kv_b = lax.all_to_all(kv_b, "zero", split_axis=0, concat_axis=0, tiled=True)
    kv_b = kv_b.reshape(-1, BLOCK, 2 * head_cols)
    kv_a = kv_b
    incoming = lax.all_to_all(
        upstream.reshape(tok_rows, seq_count, head_cols),
        "seq",
        split_axis=1,
        concat_axis=0,
        tiled=True,
    )
    local_ids = jnp.arange(local_blocks, dtype=jnp.int32)
    row_ids = (local_ids // per_shard * zero_count + zero_index) * per_shard + local_ids % per_shard
    row_lists = pattern[row_ids]
    shard_ids = row_lists // per_shard
    key_slots = (
        shard_ids % zero_count * local_blocks
        + shard_ids // zero_count * per_shard
        + row_lists % per_shard
    )

    key_slots = key_slots.reshape(local_blocks, NBK)
    slot_zero = key_slots // local_blocks
    slot_local = key_slots % local_blocks
    a_ids = jnp.where(slot_local < split, slot_zero * split + slot_local, -1)
    b_ids = slot_zero * (local_blocks - split) + jnp.maximum(slot_local - split, 0)
    out_blocks, query_grads, group_sums = block_attention(
        key_slots,
        a_ids,
        b_ids,
        queries.reshape(local_blocks, BLOCK, head_cols),
        incoming.reshape(local_blocks, BLOCK, head_cols),
        kv_a,
        kv_b,
        score_scale,
    )
    group_sums = group_sums.reshape(zero_count, local_blocks * BLOCK, 2 * head_cols)
    group_sums = lax.all_to_all(group_sums, "zero", split_axis=0, concat_axis=0, tiled=True)
    kv_sum = jnp.sum(group_sums.astype(jnp.float32), axis=0).astype(jnp.bfloat16)
    local_grads = jnp.concatenate([query_grads.reshape(-1, head_cols), kv_sum], axis=1)
    outgoing = jnp.concatenate([out_blocks.reshape(-1, head_cols), local_grads], axis=1)
    outgoing = outgoing.reshape(local_blocks * BLOCK, 4, 1, head_cols)
    token_grads = lax.all_to_all(outgoing, "seq", split_axis=0, concat_axis=2, tiled=True)
    attended = token_grads[:, 0].reshape(tok_rows, seq_count * head_cols)
    flat_grads = token_grads[:, 1:].reshape(tok_rows, 3 * seq_count * head_cols)
    g_mine = lax.dynamic_slice_in_dim(flat_grads, core * width, width, axis=1)
    g_other = lax.dynamic_slice_in_dim(flat_grads, (1 - core) * width, width, axis=1)
    token_gradient = (
        jnp.einsum("tc,dc->td", g_mine, w_mine, preferred_element_type=jnp.float32)
        + jnp.einsum("tc,dc->td", g_other, w_other, preferred_element_type=jnp.float32)
    ).astype(jnp.bfloat16)
    head_grads = local_grads
    head_part = jnp.einsum(
        "td,tc->dc", group_tokens, head_grads, preferred_element_type=jnp.float32
    )
    head_part = head_part.reshape(zero_count, -1, 3 * head_cols)
    head_part = lax.all_to_all(head_part, "zero", split_axis=0, concat_axis=0, tiled=True)
    own_rows = jnp.sum(head_part, axis=0)
    own_rows = own_rows.reshape(1, -1, 3, head_cols)
    gathered = lax.all_gather(own_rows, "seq", axis=0, tiled=True)
    weight_gradient = gathered.transpose(1, 2, 0, 3).reshape(-1, 3 * seq_count * head_cols)
    return (attended, token_gradient, weight_gradient)


def solution(mesh):
    return jax.shard_map(
        on_device,
        mesh=mesh,
        in_specs=(P(("seq", "zero"), None), P("zero", None), P(), P(("seq", "zero"), None)),
        out_specs=(P(("seq", "zero"), None), P(("seq", "zero"), None), P("zero", None)),
        check_vma=False,
    )
```

```python
import functools
import jax
import jax.numpy as jnp
from jax import lax
from jax.sharding import PartitionSpec as P
from jax.experimental import pallas as pl
from jax.experimental.pallas import tpu as pltpu

HEADS = 16
HEAD = 64
BLOCK = 128
NBK = 8
ROWS_PER_STEP = 4


def _attn_kernel(slots_ref, a_ids_ref, b_ids_ref, q_ref, up_ref, ka_ref, kb_ref, out_ref, qg_ref, kvg_ref, acc_ref, *, scale):
    i = pl.program_id(0)

    @pl.when(i == 0)
    def _():
        acc_ref[...] = jnp.zeros(acc_ref.shape, acc_ref.dtype)

    for r in range(ROWS_PER_STEP):
        row = i * ROWS_PER_STEP + r
        q = q_ref[r]
        up = up_ref[r]
        ids = [slots_ref[row, j] for j in range(NBK)]
        blocks = [
            jnp.where(a_ids_ref[row, j] >= 0, ka_ref[jnp.maximum(a_ids_ref[row, j], 0)], kb_ref[b_ids_ref[row, j]])
            for j in range(NBK)
        ]
        keys = jnp.concatenate([b[:, :HEAD] for b in blocks], axis=0)
        vals = jnp.concatenate([b[:, HEAD:] for b in blocks], axis=0)
        nt = (((1,), (1,)), ((), ()))
        tn = (((0,), (0,)), ((), ()))
        scores = lax.dot_general(q, keys, nt, preferred_element_type=jnp.float32) * scale
        row_max = jnp.max(scores, axis=-1, keepdims=True)
        exponent = jnp.exp(scores - row_max)
        prob_full = exponent / jnp.sum(exponent, axis=-1, keepdims=True)
        prob_low = prob_full.astype(jnp.bfloat16)
        out_ref[r] = jnp.dot(prob_low, vals, preferred_element_type=jnp.float32).astype(out_ref.dtype)
        prob_grad = lax.dot_general(up, vals, nt, preferred_element_type=jnp.float32)
        row_delta = jnp.sum(prob_full * prob_grad, axis=-1, keepdims=True)
        score_grad = (prob_full * (prob_grad - row_delta) * scale).astype(jnp.bfloat16)
        qg_ref[r] = jnp.dot(score_grad, keys, preferred_element_type=jnp.float32).astype(qg_ref.dtype)
        key_terms = lax.dot_general(score_grad, q, tn, preferred_element_type=jnp.float32)
        value_terms = lax.dot_general(prob_low, up, tn, preferred_element_type=jnp.float32)
        terms = jnp.concatenate([key_terms, value_terms], axis=1)
        for j in range(NBK):
            acc_ref[ids[j]] += terms[j * BLOCK:(j + 1) * BLOCK]

    @pl.when(i == pl.num_programs(0) - 1)
    def _():
        kvg_ref[...] = acc_ref[...].astype(kvg_ref.dtype)


def block_attention(slots, a_ids, b_ids, queries, upstream, kv_a, kv_b, scale):
    rows = queries.shape[0]
    slot_count = 2 * kv_a.shape[0]
    row_spec = pl.BlockSpec((ROWS_PER_STEP, BLOCK, HEAD), lambda i, s, a, b: (i, 0, 0))
    half_spec = pl.BlockSpec((slot_count // 2, BLOCK, 2 * HEAD), lambda i, s, a, b: (0, 0, 0))
    full_spec = pl.BlockSpec((slot_count, BLOCK, 2 * HEAD), lambda i, s, a, b: (0, 0, 0))
    grid_spec = pltpu.PrefetchScalarGridSpec(
        num_scalar_prefetch=3,
        grid=(rows // ROWS_PER_STEP,),
        in_specs=[row_spec, row_spec, half_spec, half_spec],
        out_specs=[row_spec, row_spec, full_spec],
        scratch_shapes=[pltpu.VMEM((slot_count, BLOCK, 2 * HEAD), jnp.float32)],
    )
    out_shape = [
        jax.ShapeDtypeStruct((rows, BLOCK, HEAD), jnp.bfloat16),
        jax.ShapeDtypeStruct((rows, BLOCK, HEAD), jnp.bfloat16),
        jax.ShapeDtypeStruct((slot_count, BLOCK, 2 * HEAD), jnp.bfloat16),
    ]
    return pl.pallas_call(
        functools.partial(_attn_kernel, scale=scale),
        grid_spec=grid_spec,
        out_shape=out_shape,
        compiler_params=pltpu.CompilerParams(
            dimension_semantics=("arbitrary",), vmem_limit_bytes=48 * 1024 * 1024
        ),
    )(slots, a_ids, b_ids, queries, upstream, kv_a, kv_b)


def on_device(tokens, projection, pattern, upstream):
    seq_count = lax.axis_size("seq")
    zero_count = lax.axis_size("zero")
    zero_index = lax.axis_index("zero")
    tok_rows = tokens.shape[0]
    model_width = tokens.shape[1]
    heads_here = HEADS // seq_count
    head_cols = heads_here * HEAD
    per_shard = tok_rows // BLOCK
    local_blocks = seq_count * per_shard
    score_scale = HEAD ** (-0.5)
    seq_index = lax.axis_index("seq")
    core = seq_index % 2
    pair = [(i, i ^ 1) for i in range(seq_count)]
    width = projection.shape[1] // 2
    w_mine = lax.dynamic_slice_in_dim(projection, core * width, width, axis=1)
    w_mine = lax.all_gather(w_mine, "zero", axis=0, tiled=True)
    w_other = lax.ppermute(w_mine, "seq", pair)
    group_tokens = lax.all_gather(tokens, "seq", axis=0, tiled=True)
    head_w = projection.reshape(projection.shape[0], 3, seq_count, head_cols)
    head_w = lax.dynamic_index_in_dim(head_w, seq_index, axis=2, keepdims=False)
    head_w = lax.all_gather(head_w, "zero", axis=0, tiled=True)
    kv_local = jnp.einsum(
        "td,dc->tc",
        group_tokens,
        head_w[:, 1:].reshape(-1, 2 * head_cols),
        preferred_element_type=jnp.float32,
    ).astype(jnp.bfloat16)
    kv_local, group_tokens, upstream = lax.optimization_barrier((kv_local, group_tokens, upstream))
    queries = jnp.einsum(
        "td,dc->tc", group_tokens, head_w[:, 0], preferred_element_type=jnp.float32
    ).astype(jnp.bfloat16)
    kv_local = kv_local.reshape(local_blocks, BLOCK, 2 * head_cols)
    split = local_blocks // 2
    kv_a = lax.all_gather(kv_local[:split], "zero", axis=0, tiled=True)
    kv_b = jnp.broadcast_to(kv_local[split:], (zero_count,) + kv_local[split:].shape)
    kv_b = lax.all_to_all(kv_b, "zero", split_axis=0, concat_axis=0, tiled=True)
    kv_b = kv_b.reshape(-1, BLOCK, 2 * head_cols)
    incoming = lax.all_to_all(
        upstream.reshape(tok_rows, seq_count, head_cols),
        "seq",
        split_axis=1,
        concat_axis=0,
        tiled=True,
    )
    local_ids = jnp.arange(local_blocks, dtype=jnp.int32)
    row_ids = (local_ids // per_shard * zero_count + zero_index) * per_shard + local_ids % per_shard
    row_lists = pattern[row_ids]
    shard_ids = row_lists // per_shard
    key_slots = (
        shard_ids % zero_count * local_blocks
        + shard_ids // zero_count * per_shard
        + row_lists % per_shard
    )

    key_slots = key_slots.reshape(local_blocks, NBK)
    slot_zero = key_slots // local_blocks
    slot_local = key_slots % local_blocks
    a_ids = jnp.where(slot_local < split, slot_zero * split + slot_local, -1)
    b_ids = slot_zero * (local_blocks - split) + jnp.maximum(slot_local - split, 0)
    out_blocks, query_grads, group_sums = block_attention(
        key_slots,
        a_ids,
        b_ids,
        queries.reshape(local_blocks, BLOCK, head_cols),
        incoming.reshape(local_blocks, BLOCK, head_cols),
        kv_a,
        kv_b,
        score_scale,
    )
    group_sums = group_sums.reshape(zero_count, local_blocks * BLOCK, 2 * head_cols)
    group_sums = lax.all_to_all(group_sums, "zero", split_axis=0, concat_axis=0, tiled=True)
    kv_sum = jnp.sum(group_sums.astype(jnp.float32), axis=0).astype(jnp.bfloat16)
    local_grads = jnp.concatenate([query_grads.reshape(-1, head_cols), kv_sum], axis=1)
    outgoing = jnp.concatenate([out_blocks.reshape(-1, head_cols), local_grads], axis=1)
    outgoing = outgoing.reshape(local_blocks * BLOCK, 4, 1, head_cols)
    token_grads = lax.all_to_all(outgoing, "seq", split_axis=0, concat_axis=2, tiled=True)
    attended = token_grads[:, 0].reshape(tok_rows, seq_count * head_cols)
    flat_grads = token_grads[:, 1:].reshape(tok_rows, 3 * seq_count * head_cols)
    g_mine = lax.dynamic_slice_in_dim(flat_grads, core * width, width, axis=1)
    g_other = lax.dynamic_slice_in_dim(flat_grads, (1 - core) * width, width, axis=1)
    token_gradient = (
        jnp.einsum("tc,dc->td", g_mine, w_mine, preferred_element_type=jnp.float32)
        + jnp.einsum("tc,dc->td", g_other, w_other, preferred_element_type=jnp.float32)
    ).astype(jnp.bfloat16)
    head_grads = local_grads
    head_part = jnp.einsum(
        "td,tc->dc", group_tokens, head_grads, preferred_element_type=jnp.float32
    )
    head_part = head_part.reshape(zero_count, -1, 3 * head_cols)
    head_part = lax.all_to_all(head_part, "zero", split_axis=0, concat_axis=0, tiled=True)
    own_rows = jnp.sum(head_part, axis=0)
    own_rows = own_rows.reshape(1, -1, 3, head_cols)
    gathered = lax.all_gather(own_rows, "seq", axis=0, tiled=True)
    weight_gradient = gathered.transpose(1, 2, 0, 3).reshape(-1, 3 * seq_count * head_cols)
    return (attended, token_gradient, weight_gradient)


def solution(mesh):
    return jax.shard_map(
        on_device,
        mesh=mesh,
        in_specs=(P(("seq", "zero"), None), P("zero", None), P(), P(("seq", "zero"), None)),
        out_specs=(P(("seq", "zero"), None), P(("seq", "zero"), None), P("zero", None)),
        check_vma=False,
    )
```

```python
import functools
import jax
import jax.numpy as jnp
from jax import lax
from jax.sharding import PartitionSpec as P
from jax.experimental import pallas as pl
from jax.experimental.pallas import tpu as pltpu

HEADS = 16
HEAD = 64
BLOCK = 128
NBK = 8
ROWS_PER_STEP = 2


def _attn_kernel(slots_ref, a_ids_ref, b_ids_ref, q_ref, up_ref, ka_ref, kb_ref, out_ref, qg_ref, kvg_ref, acc_ref, *, scale):
    i = pl.program_id(0)

    @pl.when(i == 0)
    def _():
        acc_ref[...] = jnp.zeros(acc_ref.shape, acc_ref.dtype)

    for r in range(ROWS_PER_STEP):
        row = i * ROWS_PER_STEP + r
        q = q_ref[r]
        up = up_ref[r]
        ids = [slots_ref[row, j] for j in range(NBK)]
        blocks = [
            jnp.where(a_ids_ref[row, j] >= 0, ka_ref[jnp.maximum(a_ids_ref[row, j], 0)], kb_ref[b_ids_ref[row, j]])
            for j in range(NBK)
        ]
        keys = jnp.concatenate([b[:, :HEAD] for b in blocks], axis=0)
        vals = jnp.concatenate([b[:, HEAD:] for b in blocks], axis=0)
        nt = (((1,), (1,)), ((), ()))
        tn = (((0,), (0,)), ((), ()))
        scores = lax.dot_general(q, keys, nt, preferred_element_type=jnp.float32) * scale
        row_max = jnp.max(scores, axis=-1, keepdims=True)
        exponent = jnp.exp(scores - row_max)
        prob_full = exponent / jnp.sum(exponent, axis=-1, keepdims=True)
        prob_low = prob_full.astype(jnp.bfloat16)
        out_ref[r] = jnp.dot(prob_low, vals, preferred_element_type=jnp.float32).astype(out_ref.dtype)
        prob_grad = lax.dot_general(up, vals, nt, preferred_element_type=jnp.float32)
        row_delta = jnp.sum(prob_full * prob_grad, axis=-1, keepdims=True)
        score_grad = (prob_full * (prob_grad - row_delta) * scale).astype(jnp.bfloat16)
        qg_ref[r] = jnp.dot(score_grad, keys, preferred_element_type=jnp.float32).astype(qg_ref.dtype)
        key_terms = lax.dot_general(score_grad, q, tn, preferred_element_type=jnp.float32)
        value_terms = lax.dot_general(prob_low, up, tn, preferred_element_type=jnp.float32)
        terms = jnp.concatenate([key_terms, value_terms], axis=1)
        for j in range(NBK):
            acc_ref[ids[j]] += terms[j * BLOCK:(j + 1) * BLOCK]

    @pl.when(i == pl.num_programs(0) - 1)
    def _():
        kvg_ref[...] = acc_ref[...].astype(kvg_ref.dtype)


def block_attention(slots, a_ids, b_ids, queries, upstream, kv_a, kv_b, scale):
    rows = queries.shape[0]
    slot_count = 2 * kv_a.shape[0]
    row_spec = pl.BlockSpec((ROWS_PER_STEP, BLOCK, HEAD), lambda i, s, a, b: (i, 0, 0))
    half_spec = pl.BlockSpec((slot_count // 2, BLOCK, 2 * HEAD), lambda i, s, a, b: (0, 0, 0))
    full_spec = pl.BlockSpec((slot_count, BLOCK, 2 * HEAD), lambda i, s, a, b: (0, 0, 0))
    grid_spec = pltpu.PrefetchScalarGridSpec(
        num_scalar_prefetch=3,
        grid=(rows // ROWS_PER_STEP,),
        in_specs=[row_spec, row_spec, half_spec, half_spec],
        out_specs=[row_spec, row_spec, full_spec],
        scratch_shapes=[pltpu.VMEM((slot_count, BLOCK, 2 * HEAD), jnp.float32)],
    )
    out_shape = [
        jax.ShapeDtypeStruct((rows, BLOCK, HEAD), jnp.bfloat16),
        jax.ShapeDtypeStruct((rows, BLOCK, HEAD), jnp.bfloat16),
        jax.ShapeDtypeStruct((slot_count, BLOCK, 2 * HEAD), jnp.bfloat16),
    ]
    return pl.pallas_call(
        functools.partial(_attn_kernel, scale=scale),
        grid_spec=grid_spec,
        out_shape=out_shape,
        compiler_params=pltpu.CompilerParams(
            dimension_semantics=("arbitrary",), vmem_limit_bytes=48 * 1024 * 1024
        ),
    )(slots, a_ids, b_ids, queries, upstream, kv_a, kv_b)


def on_device(tokens, projection, pattern, upstream):
    seq_count = lax.axis_size("seq")
    zero_count = lax.axis_size("zero")
    zero_index = lax.axis_index("zero")
    tok_rows = tokens.shape[0]
    model_width = tokens.shape[1]
    heads_here = HEADS // seq_count
    head_cols = heads_here * HEAD
    per_shard = tok_rows // BLOCK
    local_blocks = seq_count * per_shard
    score_scale = HEAD ** (-0.5)
    seq_index = lax.axis_index("seq")
    core = seq_index % 2
    pair = [(i, i ^ 1) for i in range(seq_count)]
    width = projection.shape[1] // 2
    w_mine = lax.dynamic_slice_in_dim(projection, core * width, width, axis=1)
    w_mine = lax.all_gather(w_mine, "zero", axis=0, tiled=True)
    w_other = lax.ppermute(w_mine, "seq", pair)
    group_tokens = lax.all_gather(tokens, "seq", axis=0, tiled=True)
    head_w = projection.reshape(projection.shape[0], 3, seq_count, head_cols)
    head_w = lax.dynamic_index_in_dim(head_w, seq_index, axis=2, keepdims=False)
    head_w = lax.all_gather(head_w, "zero", axis=0, tiled=True)
    kv_local = jnp.einsum(
        "td,dc->tc",
        group_tokens,
        head_w[:, 1:].reshape(-1, 2 * head_cols),
        preferred_element_type=jnp.float32,
    ).astype(jnp.bfloat16)
    kv_local, group_tokens, upstream = lax.optimization_barrier((kv_local, group_tokens, upstream))
    queries = jnp.einsum(
        "td,dc->tc", group_tokens, head_w[:, 0], preferred_element_type=jnp.float32
    ).astype(jnp.bfloat16)
    kv_local = kv_local.reshape(local_blocks, BLOCK, 2 * head_cols)
    split = local_blocks // 2
    kv_a = lax.all_gather(kv_local[:split], "zero", axis=0, tiled=True)
    kv_b = jnp.broadcast_to(kv_local[split:], (zero_count,) + kv_local[split:].shape)
    kv_b = lax.all_to_all(kv_b, "zero", split_axis=0, concat_axis=0, tiled=True)
    kv_b = kv_b.reshape(-1, BLOCK, 2 * head_cols)
    incoming = lax.all_to_all(
        upstream.reshape(tok_rows, seq_count, head_cols),
        "seq",
        split_axis=1,
        concat_axis=0,
        tiled=True,
    )
    local_ids = jnp.arange(local_blocks, dtype=jnp.int32)
    row_ids = (local_ids // per_shard * zero_count + zero_index) * per_shard + local_ids % per_shard
    row_lists = pattern[row_ids]
    shard_ids = row_lists // per_shard
    key_slots = (
        shard_ids % zero_count * local_blocks
        + shard_ids // zero_count * per_shard
        + row_lists % per_shard
    )

    key_slots = key_slots.reshape(local_blocks, NBK)
    slot_zero = key_slots // local_blocks
    slot_local = key_slots % local_blocks
    a_ids = jnp.where(slot_local < split, slot_zero * split + slot_local, -1)
    b_ids = slot_zero * (local_blocks - split) + jnp.maximum(slot_local - split, 0)
    out_blocks, query_grads, group_sums = block_attention(
        key_slots,
        a_ids,
        b_ids,
        queries.reshape(local_blocks, BLOCK, head_cols),
        incoming.reshape(local_blocks, BLOCK, head_cols),
        kv_a,
        kv_b,
        score_scale,
    )
    group_sums = group_sums.reshape(zero_count, local_blocks * BLOCK, 2 * head_cols)
    group_sums = lax.all_to_all(group_sums, "zero", split_axis=0, concat_axis=0, tiled=True)
    kv_sum = jnp.sum(group_sums.astype(jnp.float32), axis=0).astype(jnp.bfloat16)
    local_grads = jnp.concatenate([query_grads.reshape(-1, head_cols), kv_sum], axis=1)
    outgoing = jnp.concatenate([out_blocks.reshape(-1, head_cols), local_grads], axis=1)
    outgoing = outgoing.reshape(local_blocks * BLOCK, 4, 1, head_cols)
    token_grads = lax.all_to_all(outgoing, "seq", split_axis=0, concat_axis=2, tiled=True)
    attended = token_grads[:, 0].reshape(tok_rows, seq_count * head_cols)
    flat_grads = token_grads[:, 1:].reshape(tok_rows, 3 * seq_count * head_cols)
    g_mine = lax.dynamic_slice_in_dim(flat_grads, core * width, width, axis=1)
    g_other = lax.dynamic_slice_in_dim(flat_grads, (1 - core) * width, width, axis=1)
    token_gradient = (
        jnp.einsum("tc,dc->td", g_mine, w_mine, preferred_element_type=jnp.float32)
        + jnp.einsum("tc,dc->td", g_other, w_other, preferred_element_type=jnp.float32)
    ).astype(jnp.bfloat16)
    part_q = jnp.einsum(
        "td,tc->dc",
        group_tokens,
        query_grads.reshape(-1, head_cols),
        preferred_element_type=jnp.float32,
    )
    part_q = part_q.reshape(zero_count, -1, head_cols)
    part_q = lax.all_to_all(part_q, "zero", split_axis=0, concat_axis=0, tiled=True)
    part_kv = jnp.einsum("td,tc->dc", group_tokens, kv_sum, preferred_element_type=jnp.float32)
    part_kv = part_kv.reshape(zero_count, -1, 2 * head_cols)
    part_kv = lax.all_to_all(part_kv, "zero", split_axis=0, concat_axis=0, tiled=True)
    own_rows = jnp.concatenate([jnp.sum(part_q, axis=0), jnp.sum(part_kv, axis=0)], axis=1)
    own_rows = own_rows.reshape(1, -1, 3, head_cols)
    gathered = lax.all_gather(own_rows, "seq", axis=0, tiled=True)
    weight_gradient = gathered.transpose(1, 2, 0, 3).reshape(-1, 3 * seq_count * head_cols)
    return (attended, token_gradient, weight_gradient)


def solution(mesh):
    return jax.shard_map(
        on_device,
        mesh=mesh,
        in_specs=(P(("seq", "zero"), None), P("zero", None), P(), P(("seq", "zero"), None)),
        out_specs=(P(("seq", "zero"), None), P(("seq", "zero"), None), P("zero", None)),
        check_vma=False,
    )
```
